128 devices in a mesh: coil: 8 (over y, x_hi), pencil: 16 (over z, x_lo, core).
Axes of the slice: x: 4 (x_hi: 2, x_lo: 2; x = x_hi * 2 + x_lo), y: 4, z: 4, core: 2. Of those that a mesh axis runs over, the one named last changes fastest.
Arguments:
- object_image: bfloat16 [32, 256, 1024], P(None, 'pencil'), may hold values from -6 to 6
- coil_maps: bfloat16 [64, 32, 256, 1024], P('coil', None, 'pencil'), may hold values from -0.75 to 0.75
- sample_mask: int32 [32, 256, 4], replicated, may hold values 0 or 1
Outputs:
- adjoint_image: float32 [32, 256, 1024], P('coil', 'pencil')
The draws below stay inside these ranges and needn't reach their ends.
Inputs may be any that keep to these rules, and one draw needn't show every extreme that they name: `sample_mask`: 1 where the 128 readout samples of a segment are acquired.
All inputs are finite; a program needn't handle non-finite values.
Results may differ from the reference program's by a relative error of at most 0.01.
Values may be sent and summed in bfloat16 or wider, within the bound.
No kernel may reach another device: no remote copies, remote signals or barrier semaphores. Data moves between devices by JAX's collectives and lax.ppermute only.
A program may use at most 192 MiB of HBM per device.

```python
import math
import jax
import jax.numpy as jnp
from jax import lax

COILS = 64
SLICES = 32
NY = 256
NX = 512
SEG = 128


def touch_ends(result, key, least, largest):
    index_at = [jax.random.randint(jax.random.fold_in(key, axis), (), 0, length) for axis, length in enumerate(result.shape)]
    main_axis = result.shape.index(max(result.shape))
    neighbour = index_at[:main_axis] + [(index_at[main_axis] + 1) % result.shape[main_axis]] + index_at[main_axis + 1:]
    return result.at[tuple(index_at)].set(least).at[tuple(neighbour)].set(largest)


def block_scale(rng, dims, cuts, least, top_value):
    def one(axis_at, blocks):
        heights = jax.random.uniform(jax.random.fold_in(jax.random.fold_in(rng, 6), axis_at), (blocks,), jnp.float32, least / len(cuts), top_value / len(cuts))
        return jnp.repeat(jnp.exp(heights), dims[axis_at] // blocks).reshape((-1,) + (1,) * (len(dims) - axis_at - 1))

    level = one(*cuts[0])
    for cut in cuts[1:]:
        level = level * one(*cut)
    return level


def centred(rng, dims, width, most, split=(), kind=jnp.bfloat16):
    result = jax.random.normal(rng, dims, jnp.float32) * width
    if len(split) > 0:
        result = block_scale(rng, dims, split, -0.22, 0.18) * result
    return jnp.clip(result, min=-most, max=most).astype(kind)


def setup_inputs(seed: int = 0) -> dict:
    streams_of = jax.random.split(jax.random.key(seed), 4)
    object_image = centred(streams_of[0], (SLICES, NY, 2 * NX), 1.0, 6.0, ((1, 16),))
    coil_maps = centred(streams_of[1], (COILS, SLICES, NY, 2 * NX), COILS ** -0.5, 0.75, ((0, 8), (2, 16)))
    sample_mask = touch_ends((jax.random.randint(streams_of[2], (SLICES, NY, NX // SEG), 0, 2) < 1).astype(jnp.int32), jax.random.fold_in(streams_of[2], 1), 0, 1)
    return {"object_image": object_image, "coil_maps": coil_maps, "sample_mask": sample_mask}


def dft_tables(length, direction):
    indices = jnp.arange(length, dtype=jnp.int32)
    phases = indices[:, None] * indices[None, :] % length
    angles = phases.astype(jnp.float32) * (2.0 * math.pi / length)
    factor = 1.0 / math.sqrt(length)
    cosine = (jnp.cos(angles) * factor).astype(jnp.bfloat16)
    sine_part = (direction * jnp.sin(angles) * factor).astype(jnp.bfloat16)
    return (cosine, sine_part)

def readout_table(length, direction):
    cosine, sine_part = dft_tables(length, direction)
    upper = jnp.concatenate([cosine, sine_part], axis=1)
    lower = jnp.concatenate([-sine_part, cosine], axis=1)
    return jnp.concatenate([upper, lower], axis=0)

def complex_product(left_side, right_side, readout, conjugate):
    left_full = left_side.astype(jnp.float32)
    right_full = right_side.astype(jnp.float32)
    left_real = left_full[..., :readout]
    left_imag = left_full[..., readout:]
    if conjugate:
        left_imag = -left_imag
    right_real = right_full[..., :readout]
    right_imag = right_full[..., readout:]
    real_part = left_real * right_real - left_imag * right_imag
    imag_part = left_real * right_imag + left_imag * right_real
    return jnp.concatenate([real_part, imag_part], axis=-1)

def transform(volume, tables, formula, readout):
    cosine, sine_part = tables
    volume_full = volume.astype(jnp.float32)
    direct = jnp.einsum(formula, cosine.astype(jnp.float32), volume_full)
    crossed = jnp.einsum(formula, sine_part.astype(jnp.float32), volume_full)
    turned = jnp.concatenate([-crossed[..., readout:], crossed[..., :readout]], axis=-1)
    return (direct + turned).astype(jnp.bfloat16)

def widen(mask_part, segment):
    flags = jnp.repeat(mask_part, segment, axis=2) > 0
    return jnp.concatenate([flags, flags], axis=2)

def reference(object_image, coil_maps, sample_mask):
    readout = NX
    forward_x = readout_table(NX, -1.0).astype(jnp.float32)
    inverse_x = readout_table(NX, 1.0).astype(jnp.float32)
    forward_z = dft_tables(SLICES, -1.0)
    inverse_z = dft_tables(SLICES, 1.0)
    forward_y = dft_tables(NY, -1.0)
    inverse_y = dft_tables(NY, 1.0)
    sampled_cells = widen(sample_mask, SEG)

    def one_coil(summed, coil_map):
        coil_image = complex_product(coil_map, object_image, readout, False).astype(jnp.bfloat16)
        volume = jnp.dot(coil_image.astype(jnp.float32), forward_x, precision=lax.Precision.HIGHEST).astype(jnp.bfloat16)
        volume = transform(volume, forward_z, 'kz,zyx->kyx', readout)
        volume = transform(volume, forward_y, 'ky,zyx->zkx', readout)
        volume = jnp.where(sampled_cells, volume, jnp.zeros_like(volume))
        volume = transform(volume, inverse_y, 'ky,zyx->zkx', readout)
        volume = transform(volume, inverse_z, 'kz,zyx->kyx', readout)
        volume = jnp.dot(volume.astype(jnp.float32), inverse_x, precision=lax.Precision.HIGHEST).astype(jnp.bfloat16)
        return (summed + complex_product(coil_map, volume, readout, True), None)
    start = jnp.zeros((SLICES, NY, 2 * NX), jnp.float32)
    summed, unused = lax.scan(one_coil, start, coil_maps)
    return summed
```

```python
import math

import jax
import jax.numpy as jnp
from jax import lax
from jax.experimental import pallas as pl
from jax.experimental.pallas import tpu as pltpu
from jax.sharding import PartitionSpec as P


def dft_tables(length, direction):
    indices = jnp.arange(length, dtype=jnp.int32)
    phases = indices[:, None] * indices[None, :] % length
    angles = phases.astype(jnp.float32) * (2.0 * math.pi / length)
    factor = 1.0 / math.sqrt(length)
    cosine = (jnp.cos(angles) * factor).astype(jnp.bfloat16)
    sine_part = (direction * jnp.sin(angles) * factor).astype(jnp.bfloat16)
    return (cosine, sine_part)


def readout_table(length, direction):
    cosine, sine_part = dft_tables(length, direction)
    upper = jnp.concatenate([cosine, sine_part], axis=1)
    lower = jnp.concatenate([-sine_part, cosine], axis=1)
    return jnp.concatenate([upper, lower], axis=0)


def block_table(length, direction):
    cosine, sine_part = dft_tables(length, direction)
    upper = jnp.concatenate([cosine, -sine_part], axis=1)
    lower = jnp.concatenate([sine_part, cosine], axis=1)
    return jnp.concatenate([upper, lower], axis=0)


def slice_tables(length, direction, rows):
    cosine, sine_part = dft_tables(length, direction)
    eye = jnp.eye(rows, dtype=jnp.bfloat16)
    return jnp.kron(cosine, eye), jnp.kron(sine_part, eye)


def turn_add(direct, crossed, half):
    return jnp.concatenate(
        [direct[:, :half] - crossed[:, half:], direct[:, half:] + crossed[:, :half]], axis=1
    )


def dot32(a, b):
    return jnp.dot(a, b, preferred_element_type=jnp.float32)


PARAMS = pltpu.CompilerParams(vmem_limit_bytes=60 * 1024 * 1024)


def forward_kernel(map_ref, obj_ref, fx_ref, kc_ref, ks_ref, out_ref):
    depth, rows, width = map_ref.shape
    half = width // 2
    maps = map_ref[...].reshape(depth * rows, width).astype(jnp.float32)
    obj = obj_ref[...].reshape(depth * rows, width).astype(jnp.float32)
    m_re, m_im = maps[:, :half], maps[:, half:]
    o_re, o_im = obj[:, :half], obj[:, half:]
    image = jnp.concatenate([m_re * o_re - m_im * o_im, m_re * o_im + m_im * o_re], axis=1)
    image = image.astype(jnp.bfloat16)
    along_x = dot32(image, fx_ref[...]).astype(jnp.bfloat16)
    direct = dot32(kc_ref[...], along_x)
    crossed = dot32(ks_ref[...], along_x)
    along_z = turn_add(direct, crossed, half).astype(jnp.bfloat16)
    out_ref[...] = along_z.reshape(out_ref.shape)


def line_kernel(in_ref, mask_ref, wf_ref, wi_ref, out_ref):
    groups, rows, width = in_ref.shape
    half = width // 2
    lines = groups * rows
    volume = in_ref[...].reshape(lines, width)
    stacked = jnp.concatenate([volume[:, :half], volume[:, half:]], axis=0)
    spectrum = dot32(wf_ref[...], stacked).astype(jnp.bfloat16)
    keep = mask_ref[...] > 0
    keep = jnp.concatenate([keep, keep], axis=0)
    sampled = jnp.where(keep, spectrum, jnp.zeros_like(spectrum))
    back = dot32(wi_ref[...], sampled).astype(jnp.bfloat16)
    result = jnp.concatenate([back[:lines], back[lines:]], axis=1)
    out_ref[...] = result.reshape(out_ref.shape)


def backward_kernel(in_ref, map_ref, kc_ref, ks_ref, fx_ref, acc_ref, out_ref):
    depth, rows, width = map_ref.shape
    half = width // 2
    volume = in_ref[...].reshape(depth * rows, width)
    direct = dot32(kc_ref[...], volume)
    crossed = dot32(ks_ref[...], volume)
    back_z = turn_add(direct, crossed, half).astype(jnp.bfloat16)
    back_x = dot32(back_z, fx_ref[...]).astype(jnp.bfloat16).astype(jnp.float32)
    maps = map_ref[...].reshape(depth * rows, width).astype(jnp.float32)
    m_re, m_im = maps[:, :half], maps[:, half:]
    b_re, b_im = back_x[:, :half], back_x[:, half:]
    product = jnp.concatenate([m_re * b_re + m_im * b_im, m_re * b_im - m_im * b_re], axis=1)

    @pl.when(pl.program_id(0) == 0)
    def _():
        out_ref[...] = acc_ref[...]

    out_ref[...] += product.reshape(out_ref.shape)


def on_device(object_image, coil_maps, sample_mask):
    width = object_image.shape[2]
    readout = width // 2
    slices, rows = object_image.shape[0], object_image.shape[1]
    coils = coil_maps.shape[0]
    pencils = lax.axis_size("pencil")
    depth = slices // pencils
    lines = rows * pencils
    segment = readout // sample_mask.shape[2]
    position = lax.axis_index("pencil")

    forward_x = readout_table(readout, -1.0)
    inverse_x = readout_table(readout, 1.0)
    kc_f, ks_f = slice_tables(slices, -1.0, rows)
    kc_i, ks_i = slice_tables(slices, 1.0, rows)
    wf = block_table(lines, -1.0)
    wi = block_table(lines, 1.0)
    mask = lax.dynamic_slice_in_dim(sample_mask, position * depth, depth, 0)
    mask = jnp.repeat(mask, segment, axis=2)

    chunks = 2 if coils % 2 == 0 else 1
    per = coils // chunks
    const2 = lambda c: (0, 0)
    const3 = lambda c: (0, 0, 0)
    acc = jnp.zeros((slices, rows, width), jnp.float32)
    for chunk in range(chunks):
        start = chunk * per
        map_spec = pl.BlockSpec((None, slices, rows, width), lambda c, s=start: (c + s, 0, 0, 0))
        split = pl.pallas_call(
            forward_kernel,
            grid=(per,),
            in_specs=[
                map_spec,
                pl.BlockSpec((slices, rows, width), const3),
                pl.BlockSpec((width, width), const2),
                pl.BlockSpec((slices * rows, slices * rows), const2),
                pl.BlockSpec((slices * rows, slices * rows), const2),
            ],
            out_specs=pl.BlockSpec(
                (pencils, None, depth, rows, width), lambda c: (0, c, 0, 0, 0)
            ),
            out_shape=jax.ShapeDtypeStruct((pencils, per, depth, rows, width), jnp.bfloat16),
            compiler_params=PARAMS,
        )(coil_maps, object_image, forward_x, kc_f, ks_f)
        gathered = lax.all_to_all(split, "pencil", 0, 0, tiled=True)
        lined = pl.pallas_call(
            line_kernel,
            grid=(per, depth),
            in_specs=[
                pl.BlockSpec((pencils, None, None, rows, width), lambda c, k: (0, c, k, 0, 0)),
                pl.BlockSpec((None, lines, readout), lambda c, k: (k, 0, 0)),
                pl.BlockSpec((2 * lines, 2 * lines), lambda c, k: (0, 0)),
                pl.BlockSpec((2 * lines, 2 * lines), lambda c, k: (0, 0)),
            ],
            out_specs=pl.BlockSpec(
                (pencils, None, None, rows, width), lambda c, k: (0, c, k, 0, 0)
            ),
            out_shape=jax.ShapeDtypeStruct((pencils, per, depth, rows, width), jnp.bfloat16),
            compiler_params=PARAMS,
        )(gathered, mask, wf, wi)
        returned = lax.all_to_all(lined, "pencil", 0, 0, tiled=True)
        acc = pl.pallas_call(
            backward_kernel,
            grid=(per,),
            in_specs=[
                pl.BlockSpec((pencils, None, depth, rows, width), lambda c: (0, c, 0, 0, 0)),
                map_spec,
                pl.BlockSpec((slices * rows, slices * rows), const2),
                pl.BlockSpec((slices * rows, slices * rows), const2),
                pl.BlockSpec((width, width), const2),
                pl.BlockSpec((slices, rows, width), const3),
            ],
            out_specs=pl.BlockSpec((slices, rows, width), const3),
            out_shape=jax.ShapeDtypeStruct((slices, rows, width), jnp.float32),
            input_output_aliases={5: 0},
            compiler_params=pltpu.CompilerParams(
                vmem_limit_bytes=60 * 1024 * 1024, dimension_semantics=("arbitrary",)
            ),
        )(returned, coil_maps, kc_i, ks_i, inverse_x, acc)
    summed = lax.psum_scatter(acc.astype(jnp.bfloat16), "coil", scatter_dimension=0, tiled=True)
    return summed.astype(jnp.float32)


def solution(mesh):
    placed = (P(None, "pencil", None), P("coil", None, "pencil", None), P())
    return jax.shard_map(
        on_device, mesh=mesh, in_specs=placed, out_specs=P("coil", "pencil", None), check_vma=False
    )
```

```python
import math

import jax
import ml_dtypes
import numpy as np
import jax.numpy as jnp
from jax import lax
from jax.experimental import pallas as pl
from jax.experimental.pallas import tpu as pltpu
from jax.sharding import PartitionSpec as P


def dft_tables(length, direction):
    indices = np.arange(length, dtype=np.int32)
    phases = indices[:, None] * indices[None, :] % length
    angles = phases.astype(np.float32) * np.float32(2.0 * math.pi / length)
    factor = np.float32(1.0 / math.sqrt(length))
    cosine = (np.cos(angles) * factor).astype(ml_dtypes.bfloat16)
    sine_part = (np.float32(direction) * np.sin(angles) * factor).astype(ml_dtypes.bfloat16)
    return (cosine, sine_part)


def readout_table(length, direction):
    cosine, sine_part = dft_tables(length, direction)
    upper = np.concatenate([cosine, sine_part], axis=1)
    lower = np.concatenate([-sine_part, cosine], axis=1)
    return jnp.asarray(np.concatenate([upper, lower], axis=0))


def block_table(length, direction):
    cosine, sine_part = dft_tables(length, direction)
    upper = np.concatenate([cosine, -sine_part], axis=1)
    lower = np.concatenate([sine_part, cosine], axis=1)
    return jnp.asarray(np.concatenate([upper, lower], axis=0))


def slice_tables(length, direction, rows):
    cosine, sine_part = dft_tables(length, direction)
    eye = np.eye(rows, dtype=np.float32)
    kron = lambda t: jnp.asarray(np.kron(t.astype(np.float32), eye).astype(ml_dtypes.bfloat16))
    return kron(cosine), kron(sine_part)


def turn_add(direct, crossed, half):
    return jnp.concatenate(
        [direct[:, :half] - crossed[:, half:], direct[:, half:] + crossed[:, :half]], axis=1
    )


def dot32(a, b):
    return jnp.dot(a, b, preferred_element_type=jnp.float32)


PARAMS = pltpu.CompilerParams(vmem_limit_bytes=60 * 1024 * 1024)


def forward_kernel(map_ref, obj_ref, fx_ref, kc_ref, ks_ref, out_ref):
    depth, rows, width = map_ref.shape
    half = width // 2
    maps = map_ref[...].reshape(depth * rows, width).astype(jnp.float32)
    obj = obj_ref[...].reshape(depth * rows, width).astype(jnp.float32)
    m_re, m_im = maps[:, :half], maps[:, half:]
    o_re, o_im = obj[:, :half], obj[:, half:]
    image = jnp.concatenate([m_re * o_re - m_im * o_im, m_re * o_im + m_im * o_re], axis=1)
    image = image.astype(jnp.bfloat16)
    along_x = dot32(image, fx_ref[...]).astype(jnp.bfloat16)
    direct = dot32(kc_ref[...], along_x)
    crossed = dot32(ks_ref[...], along_x)
    along_z = turn_add(direct, crossed, half).astype(jnp.bfloat16)
    out_ref[...] = along_z.reshape(out_ref.shape)


def line_kernel(in_ref, mask_ref, wf_ref, wi_ref, out_ref):
    groups, rows, width = in_ref.shape
    half = width // 2
    lines = groups * rows
    volume = in_ref[...].reshape(lines, width)
    stacked = jnp.concatenate([volume[:, :half], volume[:, half:]], axis=0)
    spectrum = dot32(wf_ref[...], stacked).astype(jnp.bfloat16)
    keep = mask_ref[...] > 0
    keep = jnp.concatenate([keep, keep], axis=0)
    sampled = jnp.where(keep, spectrum, jnp.zeros_like(spectrum))
    back = dot32(wi_ref[...], sampled).astype(jnp.bfloat16)
    result = jnp.concatenate([back[:lines], back[lines:]], axis=1)
    out_ref[...] = result.reshape(out_ref.shape)


def backward_kernel(in_ref, map_ref, kc_ref, ks_ref, fx_ref, acc_ref, out_ref):
    depth, rows, width = map_ref.shape
    half = width // 2
    volume = in_ref[...].reshape(depth * rows, width)
    direct = dot32(kc_ref[...], volume)
    crossed = dot32(ks_ref[...], volume)
    back_z = turn_add(direct, crossed, half).astype(jnp.bfloat16)
    back_x = dot32(back_z, fx_ref[...]).astype(jnp.bfloat16).astype(jnp.float32)
    maps = map_ref[...].reshape(depth * rows, width).astype(jnp.float32)
    m_re, m_im = maps[:, :half], maps[:, half:]
    b_re, b_im = back_x[:, :half], back_x[:, half:]
    product = jnp.concatenate([m_re * b_re + m_im * b_im, m_re * b_im - m_im * b_re], axis=1)

    @pl.when(pl.program_id(0) == 0)
    def _():
        out_ref[...] = acc_ref[...]

    out_ref[...] += product.reshape(out_ref.shape)


def on_device(object_image, coil_maps, sample_mask):
    width = object_image.shape[2]
    readout = width // 2
    slices, rows = object_image.shape[0], object_image.shape[1]
    coils = coil_maps.shape[0]
    pencils = lax.axis_size("pencil")
    depth = slices // pencils
    lines = rows * pencils
    segment = readout // sample_mask.shape[2]
    position = lax.axis_index("pencil")

    forward_x = readout_table(readout, -1.0)
    inverse_x = readout_table(readout, 1.0)
    kc_f, ks_f = slice_tables(slices, -1.0, rows)
    kc_i, ks_i = slice_tables(slices, 1.0, rows)
    wf = block_table(lines, -1.0)
    wi = block_table(lines, 1.0)
    mask = lax.dynamic_slice_in_dim(sample_mask, position * depth, depth, 0)
    mask = jnp.repeat(mask, segment, axis=2)

    chunks = 2 if coils % 2 == 0 else 1
    per = coils // chunks
    const2 = lambda c: (0, 0)
    const3 = lambda c: (0, 0, 0)
    acc = jnp.zeros((slices, rows, width), jnp.float32)
    for chunk in range(chunks):
        start = chunk * per
        map_spec = pl.BlockSpec((None, slices, rows, width), lambda c, s=start: (c + s, 0, 0, 0))
        split = pl.pallas_call(
            forward_kernel,
            grid=(per,),
            in_specs=[
                map_spec,
                pl.BlockSpec((slices, rows, width), const3),
                pl.BlockSpec((width, width), const2),
                pl.BlockSpec((slices * rows, slices * rows), const2),
                pl.BlockSpec((slices * rows, slices * rows), const2),
            ],
            out_specs=pl.BlockSpec(
                (pencils, None, depth, rows, width), lambda c: (0, c, 0, 0, 0)
            ),
            out_shape=jax.ShapeDtypeStruct((pencils, per, depth, rows, width), jnp.bfloat16),
            compiler_params=PARAMS,
        )(coil_maps, object_image, forward_x, kc_f, ks_f)
        gathered = lax.all_to_all(split, "pencil", 0, 0, tiled=True)
        lined = pl.pallas_call(
            line_kernel,
            grid=(per, depth),
            in_specs=[
                pl.BlockSpec((pencils, None, None, rows, width), lambda c, k: (0, c, k, 0, 0)),
                pl.BlockSpec((None, lines, readout), lambda c, k: (k, 0, 0)),
                pl.BlockSpec((2 * lines, 2 * lines), lambda c, k: (0, 0)),
                pl.BlockSpec((2 * lines, 2 * lines), lambda c, k: (0, 0)),
            ],
            out_specs=pl.BlockSpec(
                (pencils, None, None, rows, width), lambda c, k: (0, c, k, 0, 0)
            ),
            out_shape=jax.ShapeDtypeStruct((pencils, per, depth, rows, width), jnp.bfloat16),
            compiler_params=PARAMS,
        )(gathered, mask, wf, wi)
        returned = lax.all_to_all(lined, "pencil", 0, 0, tiled=True)
        acc = pl.pallas_call(
            backward_kernel,
            grid=(per,),
            in_specs=[
                pl.BlockSpec((pencils, None, depth, rows, width), lambda c: (0, c, 0, 0, 0)),
                map_spec,
                pl.BlockSpec((slices * rows, slices * rows), const2),
                pl.BlockSpec((slices * rows, slices * rows), const2),
                pl.BlockSpec((width, width), const2),
                pl.BlockSpec((slices, rows, width), const3),
            ],
            out_specs=pl.BlockSpec((slices, rows, width), const3),
            out_shape=jax.ShapeDtypeStruct((slices, rows, width), jnp.float32),
            input_output_aliases={5: 0},
            compiler_params=pltpu.CompilerParams(
                vmem_limit_bytes=60 * 1024 * 1024, dimension_semantics=("arbitrary",)
            ),
        )(returned, coil_maps, kc_i, ks_i, inverse_x, acc)
    groups = lax.axis_size("coil")
    parts = acc.astype(jnp.bfloat16).reshape(groups, slices // groups, rows, width)
    parts = lax.all_to_all(parts, "coil", 0, 0, tiled=True)
    return jnp.sum(parts.astype(jnp.float32), axis=0)


def solution(mesh):
    placed = (P(None, "pencil", None), P("coil", None, "pencil", None), P())
    return jax.shard_map(
        on_device, mesh=mesh, in_specs=placed, out_specs=P("coil", "pencil", None), check_vma=False
    )
```

```python
import math

import jax
import ml_dtypes
import numpy as np
import jax.numpy as jnp
from jax import lax
from jax.experimental import pallas as pl
from jax.experimental.pallas import tpu as pltpu
from jax.sharding import PartitionSpec as P


def dft_tables(length, direction):
    indices = np.arange(length, dtype=np.int32)
    phases = indices[:, None] * indices[None, :] % length
    angles = phases.astype(np.float32) * np.float32(2.0 * math.pi / length)
    factor = np.float32(1.0 / math.sqrt(length))
    cosine = (np.cos(angles) * factor).astype(ml_dtypes.bfloat16)
    sine_part = (np.float32(direction) * np.sin(angles) * factor).astype(ml_dtypes.bfloat16)
    return (cosine, sine_part)


def readout_table(length, direction):
    cosine, sine_part = dft_tables(length, direction)
    upper = np.concatenate([cosine, sine_part], axis=1)
    lower = np.concatenate([-sine_part, cosine], axis=1)
    return jnp.asarray(np.concatenate([upper, lower], axis=0))


def block_table(length, direction):
    cosine, sine_part = dft_tables(length, direction)
    upper = np.concatenate([cosine, -sine_part], axis=1)
    lower = np.concatenate([sine_part, cosine], axis=1)
    return jnp.asarray(np.concatenate([upper, lower], axis=0))


def slice_tables(length, direction, rows):
    cosine, sine_part = dft_tables(length, direction)
    eye = np.eye(rows, dtype=np.float32)
    kron = lambda t: jnp.asarray(np.kron(t.astype(np.float32), eye).astype(ml_dtypes.bfloat16))
    return kron(cosine), kron(sine_part)


def turn_add(direct, crossed, half):
    return jnp.concatenate(
        [direct[:, :half] - crossed[:, half:], direct[:, half:] + crossed[:, :half]], axis=1
    )


def dot32(a, b):
    return jnp.dot(a, b, preferred_element_type=jnp.float32)


PARAMS = pltpu.CompilerParams(vmem_limit_bytes=60 * 1024 * 1024)


def forward_kernel(map_ref, obj_ref, fx_ref, kc_ref, ks_ref, out_ref):
    depth, rows, width = map_ref.shape
    half = width // 2
    maps = map_ref[...].reshape(depth * rows, width).astype(jnp.float32)
    obj = obj_ref[...].reshape(depth * rows, width).astype(jnp.float32)
    m_re, m_im = maps[:, :half], maps[:, half:]
    o_re, o_im = obj[:, :half], obj[:, half:]
    image = jnp.concatenate([m_re * o_re - m_im * o_im, m_re * o_im + m_im * o_re], axis=1)
    image = image.astype(jnp.bfloat16)
    along_x = dot32(image, fx_ref[...]).astype(jnp.bfloat16)
    direct = dot32(kc_ref[...], along_x)
    crossed = dot32(ks_ref[...], along_x)
    along_z = turn_add(direct, crossed, half).astype(jnp.bfloat16)
    out_ref[...] = along_z.reshape(out_ref.shape)


def line_kernel(in_ref, mask_ref, wf_ref, wi_ref, out_ref):
    groups, rows, width = in_ref.shape
    half = width // 2
    lines = groups * rows
    volume = in_ref[...].reshape(lines, width)
    stacked = jnp.concatenate([volume[:, :half], volume[:, half:]], axis=0)
    spectrum = dot32(wf_ref[...], stacked).astype(jnp.bfloat16)
    keep = mask_ref[...] > 0
    keep = jnp.concatenate([keep, keep], axis=0)
    sampled = jnp.where(keep, spectrum, jnp.zeros_like(spectrum))
    back = dot32(wi_ref[...], sampled).astype(jnp.bfloat16)
    result = jnp.concatenate([back[:lines], back[lines:]], axis=1)
    out_ref[...] = result.reshape(out_ref.shape)


def backward_kernel(in_ref, map_ref, kc_ref, ks_ref, fx_ref, acc_ref, out_ref):
    depth, rows, width = map_ref.shape
    half = width // 2
    volume = in_ref[...].reshape(depth * rows, width)
    direct = dot32(kc_ref[...], volume)
    crossed = dot32(ks_ref[...], volume)
    back_z = turn_add(direct, crossed, half).astype(jnp.bfloat16)
    back_x = dot32(back_z, fx_ref[...]).astype(jnp.bfloat16).astype(jnp.float32)
    maps = map_ref[...].reshape(depth * rows, width).astype(jnp.float32)
    m_re, m_im = maps[:, :half], maps[:, half:]
    b_re, b_im = back_x[:, :half], back_x[:, half:]
    product = jnp.concatenate([m_re * b_re + m_im * b_im, m_re * b_im - m_im * b_re], axis=1)

    @pl.when(pl.program_id(0) == 0)
    def _():
        out_ref[...] = acc_ref[...]

    out_ref[...] += product.reshape(out_ref.shape)


def on_device(object_image, coil_maps, sample_mask):
    width = object_image.shape[2]
    readout = width // 2
    slices, rows = object_image.shape[0], object_image.shape[1]
    coils = coil_maps.shape[0]
    pencils = lax.axis_size("pencil")
    depth = slices // pencils
    lines = rows * pencils
    segment = readout // sample_mask.shape[2]
    position = lax.axis_index("pencil")

    forward_x = readout_table(readout, -1.0)
    inverse_x = readout_table(readout, 1.0)
    kc_f, ks_f = slice_tables(slices, -1.0, rows)
    kc_i, ks_i = slice_tables(slices, 1.0, rows)
    wf = block_table(lines, -1.0)
    wi = block_table(lines, 1.0)
    mask = lax.dynamic_slice_in_dim(sample_mask, position * depth, depth, 0)
    mask = jnp.repeat(mask, segment, axis=2)

    chunks = 4 if coils % 4 == 0 else 1
    per = coils // chunks
    const2 = lambda c: (0, 0)
    const3 = lambda c: (0, 0, 0)
    acc = jnp.zeros((slices, rows, width), jnp.float32)
    for chunk in range(chunks):
        start = chunk * per
        map_spec = pl.BlockSpec((None, slices, rows, width), lambda c, s=start: (c + s, 0, 0, 0))
        split = pl.pallas_call(
            forward_kernel,
            grid=(per,),
            in_specs=[
                map_spec,
                pl.BlockSpec((slices, rows, width), const3),
                pl.BlockSpec((width, width), const2),
                pl.BlockSpec((slices * rows, slices * rows), const2),
                pl.BlockSpec((slices * rows, slices * rows), const2),
            ],
            out_specs=pl.BlockSpec(
                (pencils, None, depth, rows, width), lambda c: (0, c, 0, 0, 0)
            ),
            out_shape=jax.ShapeDtypeStruct((pencils, per, depth, rows, width), jnp.bfloat16),
            compiler_params=PARAMS,
        )(coil_maps, object_image, forward_x, kc_f, ks_f)
        gathered = lax.all_to_all(split, "pencil", 0, 0, tiled=True)
        lined = pl.pallas_call(
            line_kernel,
            grid=(per, depth),
            in_specs=[
                pl.BlockSpec((pencils, None, None, rows, width), lambda c, k: (0, c, k, 0, 0)),
                pl.BlockSpec((None, lines, readout), lambda c, k: (k, 0, 0)),
                pl.BlockSpec((2 * lines, 2 * lines), lambda c, k: (0, 0)),
                pl.BlockSpec((2 * lines, 2 * lines), lambda c, k: (0, 0)),
            ],
            out_specs=pl.BlockSpec(
                (pencils, None, None, rows, width), lambda c, k: (0, c, k, 0, 0)
            ),
            out_shape=jax.ShapeDtypeStruct((pencils, per, depth, rows, width), jnp.bfloat16),
            compiler_params=PARAMS,
        )(gathered, mask, wf, wi)
        returned = lax.all_to_all(lined, "pencil", 0, 0, tiled=True)
        acc = pl.pallas_call(
            backward_kernel,
            grid=(per,),
            in_specs=[
                pl.BlockSpec((pencils, None, depth, rows, width), lambda c: (0, c, 0, 0, 0)),
                map_spec,
                pl.BlockSpec((slices * rows, slices * rows), const2),
                pl.BlockSpec((slices * rows, slices * rows), const2),
                pl.BlockSpec((width, width), const2),
                pl.BlockSpec((slices, rows, width), const3),
            ],
            out_specs=pl.BlockSpec((slices, rows, width), const3),
            out_shape=jax.ShapeDtypeStruct((slices, rows, width), jnp.float32),
            input_output_aliases={5: 0},
            compiler_params=pltpu.CompilerParams(
                vmem_limit_bytes=60 * 1024 * 1024, dimension_semantics=("arbitrary",)
            ),
        )(returned, coil_maps, kc_i, ks_i, inverse_x, acc)
    groups = lax.axis_size("coil")
    parts = acc.astype(jnp.bfloat16).reshape(groups, slices // groups, rows, width)
    parts = lax.all_to_all(parts, "coil", 0, 0, tiled=True)
    return jnp.sum(parts.astype(jnp.float32), axis=0)


def solution(mesh):
    placed = (P(None, "pencil", None), P("coil", None, "pencil", None), P())
    return jax.shard_map(
        on_device, mesh=mesh, in_specs=placed, out_specs=P("coil", "pencil", None), check_vma=False
    )
```

```python
import math

import jax
import ml_dtypes
import numpy as np
import jax.numpy as jnp
from jax import lax
from jax.experimental import pallas as pl
from jax.experimental.pallas import tpu as pltpu
from jax.sharding import PartitionSpec as P


def dft_tables(length, direction):
    indices = np.arange(length, dtype=np.int32)
    phases = indices[:, None] * indices[None, :] % length
    angles = phases.astype(np.float32) * np.float32(2.0 * math.pi / length)
    factor = np.float32(1.0 / math.sqrt(length))
    cosine = (np.cos(angles) * factor).astype(ml_dtypes.bfloat16)
    sine_part = (np.float32(direction) * np.sin(angles) * factor).astype(ml_dtypes.bfloat16)
    return (cosine, sine_part)


def readout_table(length, direction):
    cosine, sine_part = dft_tables(length, direction)
    upper = np.concatenate([cosine, sine_part], axis=1)
    lower = np.concatenate([-sine_part, cosine], axis=1)
    return jnp.asarray(np.concatenate([upper, lower], axis=0))


def block_table(length, direction):
    cosine, sine_part = dft_tables(length, direction)
    upper = np.concatenate([cosine, -sine_part], axis=1)
    lower = np.concatenate([sine_part, cosine], axis=1)
    return jnp.asarray(np.concatenate([upper, lower], axis=0))


def slice_tables(length, direction, rows):
    cosine, sine_part = dft_tables(length, direction)
    eye = np.eye(rows, dtype=np.float32)
    kron = lambda t: jnp.asarray(np.kron(t.astype(np.float32), eye).astype(ml_dtypes.bfloat16))
    return kron(cosine), kron(sine_part)


def turn_add(direct, crossed, half):
    return jnp.concatenate(
        [direct[:, :half] - crossed[:, half:], direct[:, half:] + crossed[:, :half]], axis=1
    )


def dot32(a, b):
    return jnp.dot(a, b, preferred_element_type=jnp.float32)


PARAMS = pltpu.CompilerParams(vmem_limit_bytes=60 * 1024 * 1024)


def forward_kernel(map_ref, obj_ref, fx_ref, kc_ref, ks_ref, out_ref):
    depth, rows, width = map_ref.shape
    half = width // 2
    maps = map_ref[...].reshape(depth * rows, width).astype(jnp.float32)
    obj = obj_ref[...].reshape(depth * rows, width).astype(jnp.float32)
    m_re, m_im = maps[:, :half], maps[:, half:]
    o_re, o_im = obj[:, :half], obj[:, half:]
    image = jnp.concatenate([m_re * o_re - m_im * o_im, m_re * o_im + m_im * o_re], axis=1)
    image = image.astype(jnp.bfloat16)
    along_x = dot32(image, fx_ref[...]).astype(jnp.bfloat16)
    direct = dot32(kc_ref[...], along_x)
    crossed = dot32(ks_ref[...], along_x)
    along_z = turn_add(direct, crossed, half).astype(jnp.bfloat16)
    out_ref[...] = along_z.reshape(out_ref.shape)


def line_kernel(in_ref, mask_ref, wf_ref, wi_ref, out_ref):
    groups, rows, width = in_ref.shape
    half = width // 2
    lines = groups * rows
    volume = in_ref[...].reshape(lines, width)
    stacked = jnp.concatenate([volume[:, :half], volume[:, half:]], axis=0)
    spectrum = dot32(wf_ref[...], stacked).astype(jnp.bfloat16)
    keep = mask_ref[...] > 0
    keep = jnp.concatenate([keep, keep], axis=0)
    sampled = jnp.where(keep, spectrum, jnp.zeros_like(spectrum))
    back = dot32(wi_ref[...], sampled).astype(jnp.bfloat16)
    result = jnp.concatenate([back[:lines], back[lines:]], axis=1)
    out_ref[...] = result.reshape(out_ref.shape)


def backward_kernel(in_ref, map_ref, kc_ref, ks_ref, fx_ref, acc_ref, out_ref):
    depth, rows, width = map_ref.shape
    half = width // 2
    volume = in_ref[...].reshape(depth * rows, width)
    direct = dot32(kc_ref[...], volume)
    crossed = dot32(ks_ref[...], volume)
    back_z = turn_add(direct, crossed, half).astype(jnp.bfloat16)
    back_x = dot32(back_z, fx_ref[...]).astype(jnp.bfloat16).astype(jnp.float32)
    maps = map_ref[...].reshape(depth * rows, width).astype(jnp.float32)
    m_re, m_im = maps[:, :half], maps[:, half:]
    b_re, b_im = back_x[:, :half], back_x[:, half:]
    product = jnp.concatenate([m_re * b_re + m_im * b_im, m_re * b_im - m_im * b_re], axis=1)

    @pl.when(pl.program_id(0) == 0)
    def _():
        out_ref[...] = acc_ref[...]

    out_ref[...] += product.reshape(out_ref.shape)


def on_device(object_image, coil_maps, sample_mask):
    width = object_image.shape[2]
    readout = width // 2
    slices, rows = object_image.shape[0], object_image.shape[1]
    coils = coil_maps.shape[0]
    pencils = lax.axis_size("pencil")
    depth = slices // pencils
    lines = rows * pencils
    segment = readout // sample_mask.shape[2]
    position = lax.axis_index("pencil")

    forward_x = readout_table(readout, -1.0)
    inverse_x = readout_table(readout, 1.0)
    kc_f, ks_f = slice_tables(slices, -1.0, rows)
    kc_i, ks_i = slice_tables(slices, 1.0, rows)
    wf = block_table(lines, -1.0)
    wi = block_table(lines, 1.0)
    mask = lax.dynamic_slice_in_dim(sample_mask, position * depth, depth, 0)
    mask = jnp.repeat(mask, segment, axis=2)

    tail = coils // 4
    sizes = [coils - tail, tail] if tail > 0 else [coils]
    const2 = lambda c: (0, 0)
    const3 = lambda c: (0, 0, 0)
    acc = jnp.zeros((slices, rows, width), jnp.float32)
    start = 0
    for per in sizes:
        map_spec = pl.BlockSpec((None, slices, rows, width), lambda c, s=start: (c + s, 0, 0, 0))
        split = pl.pallas_call(
            forward_kernel,
            grid=(per,),
            in_specs=[
                map_spec,
                pl.BlockSpec((slices, rows, width), const3),
                pl.BlockSpec((width, width), const2),
                pl.BlockSpec((slices * rows, slices * rows), const2),
                pl.BlockSpec((slices * rows, slices * rows), const2),
            ],
            out_specs=pl.BlockSpec(
                (pencils, None, depth, rows, width), lambda c: (0, c, 0, 0, 0)
            ),
            out_shape=jax.ShapeDtypeStruct((pencils, per, depth, rows, width), jnp.bfloat16),
            compiler_params=PARAMS,
        )(coil_maps, object_image, forward_x, kc_f, ks_f)
        gathered = lax.all_to_all(split, "pencil", 0, 0, tiled=True)
        lined = pl.pallas_call(
            line_kernel,
            grid=(per, depth),
            in_specs=[
                pl.BlockSpec((pencils, None, None, rows, width), lambda c, k: (0, c, k, 0, 0)),
                pl.BlockSpec((None, lines, readout), lambda c, k: (k, 0, 0)),
                pl.BlockSpec((2 * lines, 2 * lines), lambda c, k: (0, 0)),
                pl.BlockSpec((2 * lines, 2 * lines), lambda c, k: (0, 0)),
            ],
            out_specs=pl.BlockSpec(
                (pencils, None, None, rows, width), lambda c, k: (0, c, k, 0, 0)
            ),
            out_shape=jax.ShapeDtypeStruct((pencils, per, depth, rows, width), jnp.bfloat16),
            compiler_params=PARAMS,
        )(gathered, mask, wf, wi)
        returned = lax.all_to_all(lined, "pencil", 0, 0, tiled=True)
        acc = pl.pallas_call(
            backward_kernel,
            grid=(per,),
            in_specs=[
                pl.BlockSpec((pencils, None, depth, rows, width), lambda c: (0, c, 0, 0, 0)),
                map_spec,
                pl.BlockSpec((slices * rows, slices * rows), const2),
                pl.BlockSpec((slices * rows, slices * rows), const2),
                pl.BlockSpec((width, width), const2),
                pl.BlockSpec((slices, rows, width), const3),
            ],
            out_specs=pl.BlockSpec((slices, rows, width), const3),
            out_shape=jax.ShapeDtypeStruct((slices, rows, width), jnp.float32),
            input_output_aliases={5: 0},
            compiler_params=pltpu.CompilerParams(
                vmem_limit_bytes=60 * 1024 * 1024, dimension_semantics=("arbitrary",)
            ),
        )(returned, coil_maps, kc_i, ks_i, inverse_x, acc)
        start += per
    groups = lax.axis_size("coil")
    parts = acc.astype(jnp.bfloat16).reshape(groups, slices // groups, rows, width)
    parts = lax.all_to_all(parts, "coil", 0, 0, tiled=True)
    return jnp.sum(parts.astype(jnp.float32), axis=0)


def solution(mesh):
    placed = (P(None, "pencil", None), P("coil", None, "pencil", None), P())
    return jax.shard_map(
        on_device, mesh=mesh, in_specs=placed, out_specs=P("coil", "pencil", None), check_vma=False
    )
```

```python
import functools
import math

import jax
import ml_dtypes
import numpy as np
import jax.numpy as jnp
from jax import lax
from jax.experimental import pallas as pl
from jax.experimental.pallas import tpu as pltpu
from jax.sharding import PartitionSpec as P


def dft_tables(length, direction):
    indices = np.arange(length, dtype=np.int32)
    phases = indices[:, None] * indices[None, :] % length
    angles = phases.astype(np.float32) * np.float32(2.0 * math.pi / length)
    factor = np.float32(1.0 / math.sqrt(length))
    cosine = (np.cos(angles) * factor).astype(ml_dtypes.bfloat16)
    sine_part = (np.float32(direction) * np.sin(angles) * factor).astype(ml_dtypes.bfloat16)
    return (cosine, sine_part)


def readout_table(length, direction):
    cosine, sine_part = dft_tables(length, direction)
    upper = np.concatenate([cosine, sine_part], axis=1)
    lower = np.concatenate([-sine_part, cosine], axis=1)
    return jnp.asarray(np.concatenate([upper, lower], axis=0))


def block_table(length, direction):
    cosine, sine_part = dft_tables(length, direction)
    upper = np.concatenate([cosine, -sine_part], axis=1)
    lower = np.concatenate([sine_part, cosine], axis=1)
    return jnp.asarray(np.concatenate([upper, lower], axis=0))


def slice_tables(length, direction, rows):
    cosine, sine_part = dft_tables(length, direction)
    eye = np.eye(rows, dtype=np.float32)
    kron = lambda t: jnp.asarray(np.kron(t.astype(np.float32), eye).astype(ml_dtypes.bfloat16))
    return kron(cosine), kron(sine_part)


def turn_add(direct, crossed, half):
    return jnp.concatenate(
        [direct[:, :half] - crossed[:, half:], direct[:, half:] + crossed[:, :half]], axis=1
    )


def dot32(a, b):
    return jnp.dot(a, b, preferred_element_type=jnp.float32)


PARAMS = pltpu.CompilerParams(vmem_limit_bytes=60 * 1024 * 1024)


def forward_kernel(map_ref, obj_ref, fx_ref, kc_ref, ks_ref, out_ref):
    depth, rows, width = map_ref.shape
    half = width // 2
    maps = map_ref[...].reshape(depth * rows, width).astype(jnp.float32)
    obj = obj_ref[...].reshape(depth * rows, width).astype(jnp.float32)
    m_re, m_im = maps[:, :half], maps[:, half:]
    o_re, o_im = obj[:, :half], obj[:, half:]
    image = jnp.concatenate([m_re * o_re - m_im * o_im, m_re * o_im + m_im * o_re], axis=1)
    image = image.astype(jnp.bfloat16)
    along_x = dot32(image, fx_ref[...]).astype(jnp.bfloat16)
    direct = dot32(kc_ref[...], along_x)
    crossed = dot32(ks_ref[...], along_x)
    along_z = turn_add(direct, crossed, half).astype(jnp.bfloat16)
    out_ref[...] = along_z.reshape(out_ref.shape)


def line_kernel(in_ref, mask_ref, wf_ref, wi_ref, out_ref):
    groups, rows, width = in_ref.shape
    half = width // 2
    lines = groups * rows
    volume = in_ref[...].reshape(lines, width)
    stacked = jnp.concatenate([volume[:, :half], volume[:, half:]], axis=0)
    spectrum = dot32(wf_ref[...], stacked).astype(jnp.bfloat16)
    flags = mask_ref[...]
    segments = flags.shape[1]
    segment = half // segments
    keep = jnp.concatenate(
        [jnp.broadcast_to(flags[:, s : s + 1], (lines, segment)) for s in range(segments)], axis=1
    )
    keep = jnp.concatenate([keep, keep], axis=0) > 0
    sampled = jnp.where(keep, spectrum, jnp.zeros_like(spectrum))
    back = dot32(wi_ref[...], sampled).astype(jnp.bfloat16)
    result = jnp.concatenate([back[:lines], back[lines:]], axis=1)
    out_ref[...] = result.reshape(out_ref.shape)


def backward_kernel(first, last, in_ref, map_ref, kc_ref, ks_ref, fx_ref, *refs):
    depth, rows, width = map_ref.shape
    half = width // 2
    volume = in_ref[...].reshape(depth * rows, width)
    direct = dot32(kc_ref[...], volume)
    crossed = dot32(ks_ref[...], volume)
    back_z = turn_add(direct, crossed, half).astype(jnp.bfloat16)
    back_x = dot32(back_z, fx_ref[...]).astype(jnp.bfloat16).astype(jnp.float32)
    maps = map_ref[...].reshape(depth * rows, width).astype(jnp.float32)
    m_re, m_im = maps[:, :half], maps[:, half:]
    b_re, b_im = back_x[:, :half], back_x[:, half:]
    product = jnp.concatenate([m_re * b_re + m_im * b_im, m_re * b_im - m_im * b_re], axis=1)
    product = product.reshape(depth, rows, width)
    refs = list(refs)
    acc_ref = None if first else refs.pop(0)
    out_ref = refs.pop(0)
    sum_ref = refs.pop(0) if last else out_ref
    step = pl.program_id(0)

    @pl.when(step == 0)
    def _():
        sum_ref[...] = product if first else acc_ref[...] + product

    @pl.when(step > 0)
    def _():
        sum_ref[...] += product

    if last:
        @pl.when(step == pl.num_programs(0) - 1)
        def _():
            out_ref[...] = sum_ref[...].astype(out_ref.dtype)


def on_device(object_image, coil_maps, sample_mask):
    width = object_image.shape[2]
    readout = width // 2
    slices, rows = object_image.shape[0], object_image.shape[1]
    coils = coil_maps.shape[0]
    pencils = lax.axis_size("pencil")
    depth = slices // pencils
    lines = rows * pencils
    position = lax.axis_index("pencil")

    forward_x = readout_table(readout, -1.0)
    inverse_x = readout_table(readout, 1.0)
    kc_f, ks_f = slice_tables(slices, -1.0, rows)
    kc_i, ks_i = slice_tables(slices, 1.0, rows)
    wf = block_table(lines, -1.0)
    wi = block_table(lines, 1.0)
    mask = lax.dynamic_slice_in_dim(sample_mask, position * depth, depth, 0)

    tail = coils // 4
    sizes = [coils - tail, tail] if tail > 0 else [coils]
    const2 = lambda c: (0, 0)
    const3 = lambda c: (0, 0, 0)
    acc = None
    start = 0
    for per in sizes:
        map_spec = pl.BlockSpec((None, slices, rows, width), lambda c, s=start: (c + s, 0, 0, 0))
        split = pl.pallas_call(
            forward_kernel,
            grid=(per,),
            in_specs=[
                map_spec,
                pl.BlockSpec((slices, rows, width), const3),
                pl.BlockSpec((width, width), const2),
                pl.BlockSpec((slices * rows, slices * rows), const2),
                pl.BlockSpec((slices * rows, slices * rows), const2),
            ],
            out_specs=pl.BlockSpec(
                (pencils, None, depth, rows, width), lambda c: (0, c, 0, 0, 0)
            ),
            out_shape=jax.ShapeDtypeStruct((pencils, per, depth, rows, width), jnp.bfloat16),
            compiler_params=PARAMS,
        )(coil_maps, object_image, forward_x, kc_f, ks_f)
        gathered = lax.all_to_all(split, "pencil", 0, 0, tiled=True)
        lined = pl.pallas_call(
            line_kernel,
            grid=(per, depth),
            in_specs=[
                pl.BlockSpec((pencils, None, None, rows, width), lambda c, k: (0, c, k, 0, 0)),
                pl.BlockSpec((None, lines, sample_mask.shape[2]), lambda c, k: (k, 0, 0)),
                pl.BlockSpec((2 * lines, 2 * lines), lambda c, k: (0, 0)),
                pl.BlockSpec((2 * lines, 2 * lines), lambda c, k: (0, 0)),
            ],
            out_specs=pl.BlockSpec(
                (pencils, None, None, rows, width), lambda c, k: (0, c, k, 0, 0)
            ),
            out_shape=jax.ShapeDtypeStruct((pencils, per, depth, rows, width), jnp.bfloat16),
            compiler_params=PARAMS,
        )(gathered, mask, wf, wi)
        returned = lax.all_to_all(lined, "pencil", 0, 0, tiled=True)
        first, last = start == 0, start + per == coils
        operands = [returned, coil_maps, kc_i, ks_i, inverse_x]
        in_specs = [
            pl.BlockSpec((pencils, None, depth, rows, width), lambda c: (0, c, 0, 0, 0)),
            map_spec,
            pl.BlockSpec((slices * rows, slices * rows), const2),
            pl.BlockSpec((slices * rows, slices * rows), const2),
            pl.BlockSpec((width, width), const2),
        ]
        if not first:
            operands.append(acc)
            in_specs.append(pl.BlockSpec((slices, rows, width), const3))
        acc = pl.pallas_call(
            functools.partial(backward_kernel, first, last),
            grid=(per,),
            in_specs=in_specs,
            out_specs=pl.BlockSpec((slices, rows, width), const3),
            out_shape=jax.ShapeDtypeStruct(
                (slices, rows, width), jnp.bfloat16 if last else jnp.float32
            ),
            scratch_shapes=[pltpu.VMEM((slices, rows, width), jnp.float32)] if last else [],
            compiler_params=pltpu.CompilerParams(
                vmem_limit_bytes=60 * 1024 * 1024, dimension_semantics=("arbitrary",)
            ),
        )(*operands)
        start += per
    groups = lax.axis_size("coil")
    parts = acc.reshape(groups, slices // groups, rows, width)
    parts = lax.all_to_all(parts, "coil", 0, 0, tiled=True)
    return jnp.sum(parts.astype(jnp.float32), axis=0)


def solution(mesh):
    placed = (P(None, "pencil", None), P("coil", None, "pencil", None), P())
    return jax.shard_map(
        on_device, mesh=mesh, in_specs=placed, out_specs=P("coil", "pencil", None), check_vma=False
    )
```

```python
import functools
import math

import jax
import ml_dtypes
import numpy as np
import jax.numpy as jnp
from jax import lax
from jax.experimental import pallas as pl
from jax.experimental.pallas import tpu as pltpu
from jax.sharding import PartitionSpec as P


def dft_tables(length, direction):
    indices = np.arange(length, dtype=np.int32)
    phases = indices[:, None] * indices[None, :] % length
    angles = phases.astype(np.float32) * np.float32(2.0 * math.pi / length)
    factor = np.float32(1.0 / math.sqrt(length))
    cosine = (np.cos(angles) * factor).astype(ml_dtypes.bfloat16)
    sine_part = (np.float32(direction) * np.sin(angles) * factor).astype(ml_dtypes.bfloat16)
    return (cosine, sine_part)


def readout_table(length, direction):
    cosine, sine_part = dft_tables(length, direction)
    upper = np.concatenate([cosine, sine_part], axis=1)
    lower = np.concatenate([-sine_part, cosine], axis=1)
    return jnp.asarray(np.concatenate([upper, lower], axis=0))


def block_table(length, direction):
    cosine, sine_part = dft_tables(length, direction)
    upper = np.concatenate([cosine, -sine_part], axis=1)
    lower = np.concatenate([sine_part, cosine], axis=1)
    return jnp.asarray(np.concatenate([upper, lower], axis=0))


def slice_tables(length, direction, rows):
    cosine, sine_part = dft_tables(length, direction)
    eye = np.eye(rows, dtype=np.float32)
    kron = lambda t: jnp.asarray(np.kron(t.astype(np.float32), eye).astype(ml_dtypes.bfloat16))
    return kron(cosine), kron(sine_part)


def turn_add(direct, crossed, half):
    return jnp.concatenate(
        [direct[:, :half] - crossed[:, half:], direct[:, half:] + crossed[:, :half]], axis=1
    )


def dot32(a, b):
    return jnp.dot(a, b, preferred_element_type=jnp.float32)


PARAMS = pltpu.CompilerParams(vmem_limit_bytes=60 * 1024 * 1024)


def forward_kernel(map_ref, obj_ref, fx_ref, kc_ref, ks_ref, out_ref):
    depth, rows, width = map_ref.shape
    half = width // 2
    maps = map_ref[...].reshape(depth * rows, width).astype(jnp.float32)
    obj = obj_ref[...].reshape(depth * rows, width).astype(jnp.float32)
    m_re, m_im = maps[:, :half], maps[:, half:]
    o_re, o_im = obj[:, :half], obj[:, half:]
    image = jnp.concatenate([m_re * o_re - m_im * o_im, m_re * o_im + m_im * o_re], axis=1)
    image = image.astype(jnp.bfloat16)
    along_x = dot32(image, fx_ref[...]).astype(jnp.bfloat16)
    direct = dot32(kc_ref[...], along_x)
    crossed = dot32(ks_ref[...], along_x)
    along_z = turn_add(direct, crossed, half).astype(jnp.bfloat16)
    out_ref[...] = along_z.reshape(out_ref.shape)


def line_kernel(aliased, in_ref, mask_ref, wf_ref, wi_ref, *refs):
    groups, rows, width = in_ref.shape
    half = width // 2
    lines = groups * rows
    volume = in_ref[...].reshape(lines, width)
    stacked = jnp.concatenate([volume[:, :half], volume[:, half:]], axis=0)
    spectrum = dot32(wf_ref[...], stacked).astype(jnp.bfloat16)
    flags = mask_ref[...]
    segments = flags.shape[1]
    segment = half // segments
    keep = jnp.concatenate(
        [jnp.broadcast_to(flags[:, s : s + 1], (lines, segment)) for s in range(segments)], axis=1
    )
    keep = jnp.concatenate([keep, keep], axis=0) > 0
    sampled = jnp.where(keep, spectrum, jnp.zeros_like(spectrum))
    back = dot32(wi_ref[...], sampled).astype(jnp.bfloat16)
    result = jnp.concatenate([back[:lines], back[lines:]], axis=1)
    out_ref = refs[-1]
    out_ref[...] = result.reshape(out_ref.shape)


def backward_kernel(first, last, in_ref, map_ref, kc_ref, ks_ref, fx_ref, *refs):
    depth, rows, width = map_ref.shape
    half = width // 2
    volume = in_ref[...].reshape(depth * rows, width)
    direct = dot32(kc_ref[...], volume)
    crossed = dot32(ks_ref[...], volume)
    back_z = turn_add(direct, crossed, half).astype(jnp.bfloat16)
    back_x = dot32(back_z, fx_ref[...]).astype(jnp.bfloat16).astype(jnp.float32)
    maps = map_ref[...].reshape(depth * rows, width).astype(jnp.float32)
    m_re, m_im = maps[:, :half], maps[:, half:]
    b_re, b_im = back_x[:, :half], back_x[:, half:]
    product = jnp.concatenate([m_re * b_re + m_im * b_im, m_re * b_im - m_im * b_re], axis=1)
    product = product.reshape(depth, rows, width)
    refs = list(refs)
    acc_ref = None if first else refs.pop(0)
    out_ref = refs.pop(0)
    sum_ref = refs.pop(0) if last else out_ref
    step = pl.program_id(0)

    @pl.when(step == 0)
    def _():
        sum_ref[...] = product if first else acc_ref[...] + product

    @pl.when(step > 0)
    def _():
        sum_ref[...] += product

    if last:
        @pl.when(step == pl.num_programs(0) - 1)
        def _():
            out_ref[...] = sum_ref[...].astype(out_ref.dtype)


def on_device(object_image, coil_maps, sample_mask):
    width = object_image.shape[2]
    readout = width // 2
    slices, rows = object_image.shape[0], object_image.shape[1]
    coils = coil_maps.shape[0]
    pencils = lax.axis_size("pencil")
    depth = slices // pencils
    lines = rows * pencils
    position = lax.axis_index("pencil")

    forward_x = readout_table(readout, -1.0)
    inverse_x = readout_table(readout, 1.0)
    kc_f, ks_f = slice_tables(slices, -1.0, rows)
    kc_i, ks_i = slice_tables(slices, 1.0, rows)
    wf = block_table(lines, -1.0)
    wi = block_table(lines, 1.0)
    mask = lax.dynamic_slice_in_dim(sample_mask, position * depth, depth, 0)

    q = coils // 4
    outgoing = [q, 2 * q, q] if q > 0 else [coils]
    incoming = [3 * q, q] if q > 0 else [coils]
    const2 = lambda c: (0, 0)
    const3 = lambda c: (0, 0, 0)

    def map_spec(start):
        return pl.BlockSpec((None, slices, rows, width), lambda c: (c + start, 0, 0, 0))

    gathered = []
    start = 0
    for per in outgoing:
        split = pl.pallas_call(
            forward_kernel,
            grid=(per,),
            in_specs=[
                map_spec(start),
                pl.BlockSpec((slices, rows, width), const3),
                pl.BlockSpec((width, width), const2),
                pl.BlockSpec((slices * rows, slices * rows), const2),
                pl.BlockSpec((slices * rows, slices * rows), const2),
            ],
            out_specs=pl.BlockSpec(
                (pencils, None, depth, rows, width), lambda c: (0, c, 0, 0, 0)
            ),
            out_shape=jax.ShapeDtypeStruct((pencils, per, depth, rows, width), jnp.bfloat16),
            compiler_params=PARAMS,
        )(coil_maps, object_image, forward_x, kc_f, ks_f)
        gathered.append((start, per, lax.all_to_all(split, "pencil", 0, 0, tiled=True)))
        start += per

    offsets = [sum(incoming[:j]) for j in range(len(incoming))]
    buffers = [None] * len(incoming)
    for start, per, volume in gathered:
        j = max(i for i in range(len(incoming)) if offsets[i] <= start)
        shift = start - offsets[j]
        operands = [volume, mask, wf, wi]
        in_specs = [
            pl.BlockSpec((pencils, None, None, rows, width), lambda c, k: (0, c, k, 0, 0)),
            pl.BlockSpec((None, lines, sample_mask.shape[2]), lambda c, k: (k, 0, 0)),
            pl.BlockSpec((2 * lines, 2 * lines), lambda c, k: (0, 0)),
            pl.BlockSpec((2 * lines, 2 * lines), lambda c, k: (0, 0)),
        ]
        aliases = {}
        if buffers[j] is not None:
            operands.append(buffers[j])
            in_specs.append(pl.BlockSpec(memory_space=pl.ANY))
            aliases = {4: 0}
        buffers[j] = pl.pallas_call(
            functools.partial(line_kernel, buffers[j] is not None),
            grid=(per, depth),
            in_specs=in_specs,
            out_specs=pl.BlockSpec(
                (pencils, None, None, rows, width), lambda c, k: (0, c + shift, k, 0, 0)
            ),
            out_shape=jax.ShapeDtypeStruct(
                (pencils, incoming[j], depth, rows, width), jnp.bfloat16
            ),
            input_output_aliases=aliases,
            compiler_params=PARAMS,
        )(*operands)

    acc = None
    for start, per, lined in zip(offsets, incoming, buffers):
        returned = lax.all_to_all(lined, "pencil", 0, 0, tiled=True)
        first, last = start == 0, start + per == coils
        operands = [returned, coil_maps, kc_i, ks_i, inverse_x]
        in_specs = [
            pl.BlockSpec((pencils, None, depth, rows, width), lambda c: (0, c, 0, 0, 0)),
            map_spec(start),
            pl.BlockSpec((slices * rows, slices * rows), const2),
            pl.BlockSpec((slices * rows, slices * rows), const2),
            pl.BlockSpec((width, width), const2),
        ]
        if not first:
            operands.append(acc)
            in_specs.append(pl.BlockSpec((slices, rows, width), const3))
        acc = pl.pallas_call(
            functools.partial(backward_kernel, first, last),
            grid=(per,),
            in_specs=in_specs,
            out_specs=pl.BlockSpec((slices, rows, width), const3),
            out_shape=jax.ShapeDtypeStruct(
                (slices, rows, width), jnp.bfloat16 if last else jnp.float32
            ),
            scratch_shapes=[pltpu.VMEM((slices, rows, width), jnp.float32)] if last else [],
            compiler_params=pltpu.CompilerParams(
                vmem_limit_bytes=60 * 1024 * 1024, dimension_semantics=("arbitrary",)
            ),
        )(*operands)
    groups = lax.axis_size("coil")
    parts = acc.reshape(groups, slices // groups, rows, width)
    parts = lax.all_to_all(parts, "coil", 0, 0, tiled=True)
    return jnp.sum(parts.astype(jnp.float32), axis=0)


def solution(mesh):
    placed = (P(None, "pencil", None), P("coil", None, "pencil", None), P())
    return jax.shard_map(
        on_device, mesh=mesh, in_specs=placed, out_specs=P("coil", "pencil", None), check_vma=False
    )
```

```python
import functools
import math

import jax
import ml_dtypes
import numpy as np
import jax.numpy as jnp
from jax import lax
from jax.experimental import pallas as pl
from jax.experimental.pallas import tpu as pltpu
from jax.sharding import PartitionSpec as P


def dft_tables(length, direction):
    indices = np.arange(length, dtype=np.int32)
    phases = indices[:, None] * indices[None, :] % length
    angles = phases.astype(np.float32) * np.float32(2.0 * math.pi / length)
    factor = np.float32(1.0 / math.sqrt(length))
    cosine = (np.cos(angles) * factor).astype(ml_dtypes.bfloat16)
    sine_part = (np.float32(direction) * np.sin(angles) * factor).astype(ml_dtypes.bfloat16)
    return (cosine, sine_part)


def readout_table(length, direction):
    cosine, sine_part = dft_tables(length, direction)
    upper = np.concatenate([cosine, sine_part], axis=1)
    lower = np.concatenate([-sine_part, cosine], axis=1)
    return jnp.asarray(np.concatenate([upper, lower], axis=0))


def block_table(length, direction):
    cosine, sine_part = dft_tables(length, direction)
    upper = np.concatenate([cosine, -sine_part], axis=1)
    lower = np.concatenate([sine_part, cosine], axis=1)
    return jnp.asarray(np.concatenate([upper, lower], axis=0))


def slice_tables(length, direction, rows):
    cosine, sine_part = dft_tables(length, direction)
    eye = np.eye(rows, dtype=np.float32)
    kron = lambda t: jnp.asarray(np.kron(t.astype(np.float32), eye).astype(ml_dtypes.bfloat16))
    return kron(cosine), kron(sine_part)


def turn_add(direct, crossed, half):
    return jnp.concatenate(
        [direct[:, :half] - crossed[:, half:], direct[:, half:] + crossed[:, :half]], axis=1
    )


def dot32(a, b):
    return jnp.dot(a, b, preferred_element_type=jnp.float32)


PARAMS = pltpu.CompilerParams(vmem_limit_bytes=60 * 1024 * 1024)


def forward_kernel(map_ref, obj_ref, kc_ref, ks_ref, out_ref):
    depth, rows, width = map_ref.shape
    half = width // 2
    maps = map_ref[...].reshape(depth * rows, width).astype(jnp.float32)
    obj = obj_ref[...].reshape(depth * rows, width).astype(jnp.float32)
    m_re, m_im = maps[:, :half], maps[:, half:]
    o_re, o_im = obj[:, :half], obj[:, half:]
    image = jnp.concatenate([m_re * o_re - m_im * o_im, m_re * o_im + m_im * o_re], axis=1)
    image = image.astype(jnp.bfloat16)
    direct = dot32(kc_ref[...], image)
    crossed = dot32(ks_ref[...], image)
    along_z = turn_add(direct, crossed, half).astype(jnp.bfloat16)
    out_ref[...] = along_z.reshape(out_ref.shape)


def line_kernel(in_ref, mask_ref, fx_ref, fxi_ref, wf_ref, wi_ref, out_ref):
    groups, rows, width = in_ref.shape
    half = width // 2
    lines = groups * rows
    volume = dot32(in_ref[...].reshape(lines, width), fx_ref[...]).astype(jnp.bfloat16)
    stacked = jnp.concatenate([volume[:, :half], volume[:, half:]], axis=0)
    spectrum = dot32(wf_ref[...], stacked).astype(jnp.bfloat16)
    flags = mask_ref[...]
    segments = flags.shape[1]
    segment = half // segments
    keep = jnp.concatenate(
        [jnp.broadcast_to(flags[:, s : s + 1], (lines, segment)) for s in range(segments)], axis=1
    )
    keep = jnp.concatenate([keep, keep], axis=0) > 0
    sampled = jnp.where(keep, spectrum, jnp.zeros_like(spectrum))
    back = dot32(wi_ref[...], sampled).astype(jnp.bfloat16)
    result = jnp.concatenate([back[:lines], back[lines:]], axis=1)
    result = dot32(result, fxi_ref[...]).astype(jnp.bfloat16)
    out_ref[...] = result.reshape(out_ref.shape)


def backward_kernel(first, last, in_ref, map_ref, kc_ref, ks_ref, *refs):
    depth, rows, width = map_ref.shape
    half = width // 2
    volume = in_ref[...].reshape(depth * rows, width)
    direct = dot32(kc_ref[...], volume)
    crossed = dot32(ks_ref[...], volume)
    back_x = turn_add(direct, crossed, half).astype(jnp.bfloat16).astype(jnp.float32)
    maps = map_ref[...].reshape(depth * rows, width).astype(jnp.float32)
    m_re, m_im = maps[:, :half], maps[:, half:]
    b_re, b_im = back_x[:, :half], back_x[:, half:]
    product = jnp.concatenate([m_re * b_re + m_im * b_im, m_re * b_im - m_im * b_re], axis=1)
    product = product.reshape(depth, rows, width)
    refs = list(refs)
    acc_ref = None if first else refs.pop(0)
    out_ref = refs.pop(0)
    sum_ref = refs.pop(0) if last else out_ref
    step = pl.program_id(0)

    @pl.when(step == 0)
    def _():
        sum_ref[...] = product if first else acc_ref[...] + product

    @pl.when(step > 0)
    def _():
        sum_ref[...] += product

    if last:
        @pl.when(step == pl.num_programs(0) - 1)
        def _():
            out_ref[...] = sum_ref[...].astype(out_ref.dtype)


def on_device(object_image, coil_maps, sample_mask):
    width = object_image.shape[2]
    readout = width // 2
    slices, rows = object_image.shape[0], object_image.shape[1]
    coils = coil_maps.shape[0]
    pencils = lax.axis_size("pencil")
    depth = slices // pencils
    lines = rows * pencils
    position = lax.axis_index("pencil")

    forward_x = readout_table(readout, -1.0)
    inverse_x = readout_table(readout, 1.0)
    kc_f, ks_f = slice_tables(slices, -1.0, rows)
    kc_i, ks_i = slice_tables(slices, 1.0, rows)
    wf = block_table(lines, -1.0)
    wi = block_table(lines, 1.0)
    mask = lax.dynamic_slice_in_dim(sample_mask, position * depth, depth, 0)

    tail = (3 * coils) // 8
    sizes = [coils - tail, tail] if tail > 0 else [coils]
    const2 = lambda c: (0, 0)
    const3 = lambda c: (0, 0, 0)
    acc = None
    start = 0
    for per in sizes:
        map_spec = pl.BlockSpec((None, slices, rows, width), lambda c, s=start: (c + s, 0, 0, 0))
        split = pl.pallas_call(
            forward_kernel,
            grid=(per,),
            in_specs=[
                map_spec,
                pl.BlockSpec((slices, rows, width), const3),
                pl.BlockSpec((slices * rows, slices * rows), const2),
                pl.BlockSpec((slices * rows, slices * rows), const2),
            ],
            out_specs=pl.BlockSpec(
                (pencils, None, depth, rows, width), lambda c: (0, c, 0, 0, 0)
            ),
            out_shape=jax.ShapeDtypeStruct((pencils, per, depth, rows, width), jnp.bfloat16),
            compiler_params=PARAMS,
        )(coil_maps, object_image, kc_f, ks_f)
        gathered = lax.all_to_all(split, "pencil", 0, 0, tiled=True)
        lined = pl.pallas_call(
            line_kernel,
            grid=(per, depth),
            in_specs=[
                pl.BlockSpec((pencils, None, None, rows, width), lambda c, k: (0, c, k, 0, 0)),
                pl.BlockSpec((None, lines, sample_mask.shape[2]), lambda c, k: (k, 0, 0)),
                pl.BlockSpec((width, width), lambda c, k: (0, 0)),
                pl.BlockSpec((width, width), lambda c, k: (0, 0)),
                pl.BlockSpec((2 * lines, 2 * lines), lambda c, k: (0, 0)),
                pl.BlockSpec((2 * lines, 2 * lines), lambda c, k: (0, 0)),
            ],
            out_specs=pl.BlockSpec(
                (pencils, None, None, rows, width), lambda c, k: (0, c, k, 0, 0)
            ),
            out_shape=jax.ShapeDtypeStruct((pencils, per, depth, rows, width), jnp.bfloat16),
            compiler_params=PARAMS,
        )(gathered, mask, forward_x, inverse_x, wf, wi)
        returned = lax.all_to_all(lined, "pencil", 0, 0, tiled=True)
        first, last = start == 0, start + per == coils
        operands = [returned, coil_maps, kc_i, ks_i]
        in_specs = [
            pl.BlockSpec((pencils, None, depth, rows, width), lambda c: (0, c, 0, 0, 0)),
            map_spec,
            pl.BlockSpec((slices * rows, slices * rows), const2),
            pl.BlockSpec((slices * rows, slices * rows), const2),
        ]
        if not first:
            operands.append(acc)
            in_specs.append(pl.BlockSpec((slices, rows, width), const3))
        acc = pl.pallas_call(
            functools.partial(backward_kernel, first, last),
            grid=(per,),
            in_specs=in_specs,
            out_specs=pl.BlockSpec((slices, rows, width), const3),
            out_shape=jax.ShapeDtypeStruct(
                (slices, rows, width), jnp.bfloat16 if last else jnp.float32
            ),
            scratch_shapes=[pltpu.VMEM((slices, rows, width), jnp.float32)] if last else [],
            compiler_params=pltpu.CompilerParams(
                vmem_limit_bytes=60 * 1024 * 1024, dimension_semantics=("arbitrary",)
            ),
        )(*operands)
        start += per
    groups = lax.axis_size("coil")
    parts = acc.reshape(groups, slices // groups, rows, width)
    parts = lax.all_to_all(parts, "coil", 0, 0, tiled=True)
    return jnp.sum(parts.astype(jnp.float32), axis=0)


def solution(mesh):
    placed = (P(None, "pencil", None), P("coil", None, "pencil", None), P())
    return jax.shard_map(
        on_device, mesh=mesh, in_specs=placed, out_specs=P("coil", "pencil", None), check_vma=False
    )
```

```python
import functools
import math

import jax
import ml_dtypes
import numpy as np
import jax.numpy as jnp
from jax import lax
from jax.experimental import pallas as pl
from jax.experimental.pallas import tpu as pltpu
from jax.sharding import PartitionSpec as P


def dft_tables(length, direction):
    indices = np.arange(length, dtype=np.int32)
    phases = indices[:, None] * indices[None, :] % length
    angles = phases.astype(np.float32) * np.float32(2.0 * math.pi / length)
    factor = np.float32(1.0 / math.sqrt(length))
    cosine = (np.cos(angles) * factor).astype(ml_dtypes.bfloat16)
    sine_part = (np.float32(direction) * np.sin(angles) * factor).astype(ml_dtypes.bfloat16)
    return (cosine, sine_part)


def readout_table(length, direction):
    cosine, sine_part = dft_tables(length, direction)
    upper = np.concatenate([cosine, sine_part], axis=1)
    lower = np.concatenate([-sine_part, cosine], axis=1)
    return jnp.asarray(np.concatenate([upper, lower], axis=0))


def block_table(length, direction):
    cosine, sine_part = dft_tables(length, direction)
    upper = np.concatenate([cosine, -sine_part], axis=1)
    lower = np.concatenate([sine_part, cosine], axis=1)
    return jnp.asarray(np.concatenate([upper, lower], axis=0))


def slice_tables(length, direction, rows):
    cosine, sine_part = dft_tables(length, direction)
    eye = np.eye(rows, dtype=np.float32)
    kron = lambda t: jnp.asarray(np.kron(t.astype(np.float32), eye).astype(ml_dtypes.bfloat16))
    return kron(cosine), kron(sine_part)


def turn_add(direct, crossed, half):
    return jnp.concatenate(
        [direct[:, :half] - crossed[:, half:], direct[:, half:] + crossed[:, :half]], axis=1
    )


def dot32(a, b):
    return jnp.dot(a, b, preferred_element_type=jnp.float32)


PARAMS = pltpu.CompilerParams(vmem_limit_bytes=60 * 1024 * 1024)


def forward_kernel(map_ref, obj_ref, kc_ref, ks_ref, out_ref):
    depth, rows, width = map_ref.shape
    half = width // 2
    maps = map_ref[...].reshape(depth * rows, width).astype(jnp.float32)
    obj = obj_ref[...].reshape(depth * rows, width).astype(jnp.float32)
    m_re, m_im = maps[:, :half], maps[:, half:]
    o_re, o_im = obj[:, :half], obj[:, half:]
    image = jnp.concatenate([m_re * o_re - m_im * o_im, m_re * o_im + m_im * o_re], axis=1)
    image = image.astype(jnp.bfloat16)
    direct = dot32(kc_ref[...], image)
    crossed = dot32(ks_ref[...], image)
    along_z = turn_add(direct, crossed, half).astype(jnp.bfloat16)
    out_ref[...] = along_z.reshape(out_ref.shape)


def line_kernel(in_ref, mask_ref, fx_ref, fxi_ref, wf_ref, wi_ref, out_ref):
    groups, rows, width = in_ref.shape
    half = width // 2
    lines = groups * rows
    volume = dot32(in_ref[...].reshape(lines, width), fx_ref[...]).astype(jnp.bfloat16)
    stacked = jnp.concatenate([volume[:, :half], volume[:, half:]], axis=0)
    spectrum = dot32(wf_ref[...], stacked).astype(jnp.bfloat16)
    flags = mask_ref[...]
    segments = flags.shape[1]
    segment = half // segments
    keep = jnp.concatenate(
        [jnp.broadcast_to(flags[:, s : s + 1], (lines, segment)) for s in range(segments)], axis=1
    )
    keep = jnp.concatenate([keep, keep], axis=0) > 0
    sampled = jnp.where(keep, spectrum, jnp.zeros_like(spectrum))
    back = dot32(wi_ref[...], sampled).astype(jnp.bfloat16)
    result = jnp.concatenate([back[:lines], back[lines:]], axis=1)
    result = dot32(result, fxi_ref[...]).astype(jnp.bfloat16)
    out_ref[...] = result.reshape(out_ref.shape)


def backward_kernel(first, last, in_ref, map_ref, kc_ref, ks_ref, *refs):
    depth, rows, width = map_ref.shape
    half = width // 2
    volume = in_ref[...].reshape(depth * rows, width)
    direct = dot32(kc_ref[...], volume)
    crossed = dot32(ks_ref[...], volume)
    back_x = turn_add(direct, crossed, half).astype(jnp.bfloat16).astype(jnp.float32)
    maps = map_ref[...].reshape(depth * rows, width).astype(jnp.float32)
    m_re, m_im = maps[:, :half], maps[:, half:]
    b_re, b_im = back_x[:, :half], back_x[:, half:]
    product = jnp.concatenate([m_re * b_re + m_im * b_im, m_re * b_im - m_im * b_re], axis=1)
    product = product.reshape(depth, rows, width)
    refs = list(refs)
    acc_ref = None if first else refs.pop(0)
    out_ref = refs.pop(0)
    sum_ref = refs.pop(0) if last else out_ref
    step = pl.program_id(0)

    @pl.when(step == 0)
    def _():
        sum_ref[...] = product if first else acc_ref[...] + product

    @pl.when(step > 0)
    def _():
        sum_ref[...] += product

    if last:
        @pl.when(step == pl.num_programs(0) - 1)
        def _():
            out_ref[...] = sum_ref[...].astype(out_ref.dtype)


def on_device(object_image, coil_maps, sample_mask):
    width = object_image.shape[2]
    readout = width // 2
    slices, rows = object_image.shape[0], object_image.shape[1]
    coils = coil_maps.shape[0]
    pencils = lax.axis_size("pencil")
    depth = slices // pencils
    lines = rows * pencils
    position = lax.axis_index("pencil")

    forward_x = readout_table(readout, -1.0)
    inverse_x = readout_table(readout, 1.0)
    kc_f, ks_f = slice_tables(slices, -1.0, rows)
    kc_i, ks_i = slice_tables(slices, 1.0, rows)
    wf = block_table(lines, -1.0)
    wi = block_table(lines, 1.0)
    mask = lax.dynamic_slice_in_dim(sample_mask, position * depth, depth, 0)

    tail = coils // 2
    sizes = [coils - tail, tail] if tail > 0 else [coils]
    const2 = lambda c: (0, 0)
    const3 = lambda c: (0, 0, 0)
    acc = None
    start = 0
    for per in sizes:
        map_spec = pl.BlockSpec((None, slices, rows, width), lambda c, s=start: (c + s, 0, 0, 0))
        split = pl.pallas_call(
            forward_kernel,
            grid=(per,),
            in_specs=[
                map_spec,
                pl.BlockSpec((slices, rows, width), const3),
                pl.BlockSpec((slices * rows, slices * rows), const2),
                pl.BlockSpec((slices * rows, slices * rows), const2),
            ],
            out_specs=pl.BlockSpec(
                (pencils, None, depth, rows, width), lambda c: (0, c, 0, 0, 0)
            ),
            out_shape=jax.ShapeDtypeStruct((pencils, per, depth, rows, width), jnp.bfloat16),
            compiler_params=PARAMS,
        )(coil_maps, object_image, kc_f, ks_f)
        gathered = lax.all_to_all(split, "pencil", 0, 0, tiled=True)
        lined = pl.pallas_call(
            line_kernel,
            grid=(per, depth),
            in_specs=[
                pl.BlockSpec((pencils, None, None, rows, width), lambda c, k: (0, c, k, 0, 0)),
                pl.BlockSpec((None, lines, sample_mask.shape[2]), lambda c, k: (k, 0, 0)),
                pl.BlockSpec((width, width), lambda c, k: (0, 0)),
                pl.BlockSpec((width, width), lambda c, k: (0, 0)),
                pl.BlockSpec((2 * lines, 2 * lines), lambda c, k: (0, 0)),
                pl.BlockSpec((2 * lines, 2 * lines), lambda c, k: (0, 0)),
            ],
            out_specs=pl.BlockSpec(
                (pencils, None, None, rows, width), lambda c, k: (0, c, k, 0, 0)
            ),
            out_shape=jax.ShapeDtypeStruct((pencils, per, depth, rows, width), jnp.bfloat16),
            compiler_params=PARAMS,
        )(gathered, mask, forward_x, inverse_x, wf, wi)
        returned = lax.all_to_all(lined, "pencil", 0, 0, tiled=True)
        first, last = start == 0, start + per == coils
        operands = [returned, coil_maps, kc_i, ks_i]
        in_specs = [
            pl.BlockSpec((pencils, None, depth, rows, width), lambda c: (0, c, 0, 0, 0)),
            map_spec,
            pl.BlockSpec((slices * rows, slices * rows), const2),
            pl.BlockSpec((slices * rows, slices * rows), const2),
        ]
        if not first:
            operands.append(acc)
            in_specs.append(pl.BlockSpec((slices, rows, width), const3))
        acc = pl.pallas_call(
            functools.partial(backward_kernel, first, last),
            grid=(per,),
            in_specs=in_specs,
            out_specs=pl.BlockSpec((slices, rows, width), const3),
            out_shape=jax.ShapeDtypeStruct(
                (slices, rows, width), jnp.bfloat16 if last else jnp.float32
            ),
            scratch_shapes=[pltpu.VMEM((slices, rows, width), jnp.float32)] if last else [],
            compiler_params=pltpu.CompilerParams(
                vmem_limit_bytes=60 * 1024 * 1024, dimension_semantics=("arbitrary",)
            ),
        )(*operands)
        start += per
    groups = lax.axis_size("coil")
    parts = acc.reshape(groups, slices // groups, rows, width)
    parts = lax.all_to_all(parts, "coil", 0, 0, tiled=True)
    return jnp.sum(parts.astype(jnp.float32), axis=0)


def solution(mesh):
    placed = (P(None, "pencil", None), P("coil", None, "pencil", None), P())
    return jax.shard_map(
        on_device, mesh=mesh, in_specs=placed, out_specs=P("coil", "pencil", None), check_vma=False
    )
```

```python
import functools
import math

import jax
import ml_dtypes
import numpy as np
import jax.numpy as jnp
from jax import lax
from jax.experimental import pallas as pl
from jax.experimental.pallas import tpu as pltpu
from jax.sharding import PartitionSpec as P


def dft_tables(length, direction):
    indices = np.arange(length, dtype=np.int32)
    phases = indices[:, None] * indices[None, :] % length
    angles = phases.astype(np.float32) * np.float32(2.0 * math.pi / length)
    factor = np.float32(1.0 / math.sqrt(length))
    cosine = (np.cos(angles) * factor).astype(ml_dtypes.bfloat16)
    sine_part = (np.float32(direction) * np.sin(angles) * factor).astype(ml_dtypes.bfloat16)
    return (cosine, sine_part)


def readout_table(length, direction):
    cosine, sine_part = dft_tables(length, direction)
    upper = np.concatenate([cosine, sine_part], axis=1)
    lower = np.concatenate([-sine_part, cosine], axis=1)
    return jnp.asarray(np.concatenate([upper, lower], axis=0))


def block_table(length, direction):
    cosine, sine_part = dft_tables(length, direction)
    upper = np.concatenate([cosine, -sine_part], axis=1)
    lower = np.concatenate([sine_part, cosine], axis=1)
    return jnp.asarray(np.concatenate([upper, lower], axis=0))


def slice_tables(length, direction, rows):
    cosine, sine_part = dft_tables(length, direction)
    eye = np.eye(rows, dtype=np.float32)
    kron = lambda t: jnp.asarray(np.kron(t.astype(np.float32), eye).astype(ml_dtypes.bfloat16))
    return kron(cosine), kron(sine_part)


def turn_add(direct, crossed, half):
    return jnp.concatenate(
        [direct[:, :half] - crossed[:, half:], direct[:, half:] + crossed[:, :half]], axis=1
    )


def dot32(a, b):
    return jnp.dot(a, b, preferred_element_type=jnp.float32)


PARAMS = pltpu.CompilerParams(vmem_limit_bytes=60 * 1024 * 1024)


def forward_kernel(map_ref, obj_ref, kc_ref, ks_ref, out_ref):
    depth, rows, width = map_ref.shape
    half = width // 2
    band = kc_ref.shape[0] // depth
    maps = map_ref[...].astype(jnp.float32)
    obj = obj_ref[...].astype(jnp.float32)
    m_re, m_im = maps[..., :half], maps[..., half:]
    o_re, o_im = obj[..., :half], obj[..., half:]
    image = jnp.concatenate([m_re * o_re - m_im * o_im, m_re * o_im + m_im * o_re], axis=-1)
    pieces = []
    for h in range(rows // band):
        part = image[:, h * band : (h + 1) * band, :].reshape(depth * band, width)
        part = part.astype(jnp.bfloat16)
        direct = dot32(kc_ref[...], part)
        crossed = dot32(ks_ref[...], part)
        along_z = turn_add(direct, crossed, half).astype(jnp.bfloat16).astype(jnp.float32)
        pieces.append(along_z.reshape(depth, band, width))
    along_z = jnp.concatenate(pieces, axis=1).astype(jnp.bfloat16)
    out_ref[...] = along_z.reshape(out_ref.shape)


def line_kernel(in_ref, mask_ref, fx_ref, fxi_ref, wf_ref, wi_ref, out_ref):
    groups, rows, width = in_ref.shape
    half = width // 2
    lines = groups * rows
    volume = dot32(in_ref[...].reshape(lines, width), fx_ref[...]).astype(jnp.bfloat16)
    stacked = jnp.concatenate([volume[:, :half], volume[:, half:]], axis=0)
    spectrum = dot32(wf_ref[...], stacked).astype(jnp.bfloat16)
    flags = mask_ref[...]
    segments = flags.shape[1]
    segment = half // segments
    keep = jnp.concatenate(
        [jnp.broadcast_to(flags[:, s : s + 1], (lines, segment)) for s in range(segments)], axis=1
    )
    keep = jnp.concatenate([keep, keep], axis=0) > 0
    sampled = jnp.where(keep, spectrum, jnp.zeros_like(spectrum))
    back = dot32(wi_ref[...], sampled).astype(jnp.bfloat16)
    result = jnp.concatenate([back[:lines], back[lines:]], axis=1)
    result = dot32(result, fxi_ref[...]).astype(jnp.bfloat16)
    out_ref[...] = result.reshape(out_ref.shape)


def backward_kernel(first, last, in_ref, map_ref, kc_ref, ks_ref, *refs):
    depth, rows, width = map_ref.shape
    half = width // 2
    band = kc_ref.shape[0] // depth
    volume = in_ref[...].reshape(depth, rows, width).astype(jnp.float32)
    maps = map_ref[...].astype(jnp.float32)
    pieces = []
    for h in range(rows // band):
        part = volume[:, h * band : (h + 1) * band, :].reshape(depth * band, width)
        part = part.astype(jnp.bfloat16)
        direct = dot32(kc_ref[...], part)
        crossed = dot32(ks_ref[...], part)
        back_x = turn_add(direct, crossed, half).astype(jnp.bfloat16).astype(jnp.float32)
        coil = maps[:, h * band : (h + 1) * band, :].reshape(depth * band, width)
        m_re, m_im = coil[:, :half], coil[:, half:]
        b_re, b_im = back_x[:, :half], back_x[:, half:]
        piece = jnp.concatenate(
            [m_re * b_re + m_im * b_im, m_re * b_im - m_im * b_re], axis=1
        )
        pieces.append(piece.reshape(depth, band, width))
    product = jnp.concatenate(pieces, axis=1)
    refs = list(refs)
    acc_ref = None if first else refs.pop(0)
    out_ref = refs.pop(0)
    sum_ref = refs.pop(0) if last else out_ref
    step = pl.program_id(0)

    @pl.when(step == 0)
    def _():
        sum_ref[...] = product if first else acc_ref[...] + product

    @pl.when(step > 0)
    def _():
        sum_ref[...] += product

    if last:
        @pl.when(step == pl.num_programs(0) - 1)
        def _():
            out_ref[...] = sum_ref[...].astype(out_ref.dtype)


def on_device(object_image, coil_maps, sample_mask):
    width = object_image.shape[2]
    readout = width // 2
    slices, rows = object_image.shape[0], object_image.shape[1]
    coils = coil_maps.shape[0]
    pencils = lax.axis_size("pencil")
    depth = slices // pencils
    lines = rows * pencils
    position = lax.axis_index("pencil")

    forward_x = readout_table(readout, -1.0)
    inverse_x = readout_table(readout, 1.0)
    band = 8 if rows % 8 == 0 else rows
    kc_f, ks_f = slice_tables(slices, -1.0, band)
    kc_i, ks_i = slice_tables(slices, 1.0, band)
    wf = block_table(lines, -1.0)
    wi = block_table(lines, 1.0)
    mask = lax.dynamic_slice_in_dim(sample_mask, position * depth, depth, 0)

    tail = coils // 2
    sizes = [coils - tail, tail] if tail > 0 else [coils]
    const2 = lambda c: (0, 0)
    const3 = lambda c: (0, 0, 0)
    acc = None
    start = 0
    for per in sizes:
        map_spec = pl.BlockSpec((None, slices, rows, width), lambda c, s=start: (c + s, 0, 0, 0))
        split = pl.pallas_call(
            forward_kernel,
            grid=(per,),
            in_specs=[
                map_spec,
                pl.BlockSpec((slices, rows, width), const3),
                pl.BlockSpec((slices * band, slices * band), const2),
                pl.BlockSpec((slices * band, slices * band), const2),
            ],
            out_specs=pl.BlockSpec(
                (pencils, None, depth, rows, width), lambda c: (0, c, 0, 0, 0)
            ),
            out_shape=jax.ShapeDtypeStruct((pencils, per, depth, rows, width), jnp.bfloat16),
            compiler_params=PARAMS,
        )(coil_maps, object_image, kc_f, ks_f)
        gathered = lax.all_to_all(split, "pencil", 0, 0, tiled=True)
        lined = pl.pallas_call(
            line_kernel,
            grid=(per, depth),
            in_specs=[
                pl.BlockSpec((pencils, None, None, rows, width), lambda c, k: (0, c, k, 0, 0)),
                pl.BlockSpec((None, lines, sample_mask.shape[2]), lambda c, k: (k, 0, 0)),
                pl.BlockSpec((width, width), lambda c, k: (0, 0)),
                pl.BlockSpec((width, width), lambda c, k: (0, 0)),
                pl.BlockSpec((2 * lines, 2 * lines), lambda c, k: (0, 0)),
                pl.BlockSpec((2 * lines, 2 * lines), lambda c, k: (0, 0)),
            ],
            out_specs=pl.BlockSpec(
                (pencils, None, None, rows, width), lambda c, k: (0, c, k, 0, 0)
            ),
            out_shape=jax.ShapeDtypeStruct((pencils, per, depth, rows, width), jnp.bfloat16),
            compiler_params=PARAMS,
        )(gathered, mask, forward_x, inverse_x, wf, wi)
        returned = lax.all_to_all(lined, "pencil", 0, 0, tiled=True)
        first, last = start == 0, start + per == coils
        operands = [returned, coil_maps, kc_i, ks_i]
        in_specs = [
            pl.BlockSpec((pencils, None, depth, rows, width), lambda c: (0, c, 0, 0, 0)),
            map_spec,
            pl.BlockSpec((slices * band, slices * band), const2),
            pl.BlockSpec((slices * band, slices * band), const2),
        ]
        if not first:
            operands.append(acc)
            in_specs.append(pl.BlockSpec((slices, rows, width), const3))
        acc = pl.pallas_call(
            functools.partial(backward_kernel, first, last),
            grid=(per,),
            in_specs=in_specs,
            out_specs=pl.BlockSpec((slices, rows, width), const3),
            out_shape=jax.ShapeDtypeStruct(
                (slices, rows, width), jnp.bfloat16 if last else jnp.float32
            ),
            scratch_shapes=[pltpu.VMEM((slices, rows, width), jnp.float32)] if last else [],
            compiler_params=pltpu.CompilerParams(
                vmem_limit_bytes=60 * 1024 * 1024, dimension_semantics=("arbitrary",)
            ),
        )(*operands)
        start += per
    groups = lax.axis_size("coil")
    parts = acc.reshape(groups, slices // groups, rows, width)
    parts = lax.all_to_all(parts, "coil", 0, 0, tiled=True)
    return jnp.sum(parts.astype(jnp.float32), axis=0)


def solution(mesh):
    placed = (P(None, "pencil", None), P("coil", None, "pencil", None), P())
    return jax.shard_map(
        on_device, mesh=mesh, in_specs=placed, out_specs=P("coil", "pencil", None), check_vma=False
    )
```

```python
import functools
import math

import jax
import ml_dtypes
import numpy as np
import jax.numpy as jnp
from jax import lax
from jax.experimental import pallas as pl
from jax.experimental.pallas import tpu as pltpu
from jax.sharding import PartitionSpec as P


def dft_tables(length, direction):
    indices = np.arange(length, dtype=np.int32)
    phases = indices[:, None] * indices[None, :] % length
    angles = phases.astype(np.float32) * np.float32(2.0 * math.pi / length)
    factor = np.float32(1.0 / math.sqrt(length))
    cosine = (np.cos(angles) * factor).astype(ml_dtypes.bfloat16)
    sine_part = (np.float32(direction) * np.sin(angles) * factor).astype(ml_dtypes.bfloat16)
    return (cosine, sine_part)


def complex_tables(length):
    cosine, sine_part = dft_tables(length, -1.0)
    return lax.optimization_barrier((jnp.asarray(cosine), jnp.asarray(sine_part)))


def readout_table(cosine, sine_part):
    upper = jnp.concatenate([cosine, sine_part], axis=1)
    lower = jnp.concatenate([-sine_part, cosine], axis=1)
    return jnp.concatenate([upper, lower], axis=0)


def block_table(cosine, sine_part):
    upper = jnp.concatenate([cosine, -sine_part], axis=1)
    lower = jnp.concatenate([sine_part, cosine], axis=1)
    return jnp.concatenate([upper, lower], axis=0)


def slice_tables(length, direction, rows):
    cosine, sine_part = dft_tables(length, direction)
    eye = np.eye(rows, dtype=np.float32)
    kron = lambda t: jnp.asarray(np.kron(t.astype(np.float32), eye).astype(ml_dtypes.bfloat16))
    return kron(cosine), kron(sine_part)


def turn_add(direct, crossed, half):
    return jnp.concatenate(
        [direct[:, :half] - crossed[:, half:], direct[:, half:] + crossed[:, :half]], axis=1
    )


def dot32(a, b):
    return jnp.dot(a, b, preferred_element_type=jnp.float32)


PARAMS = pltpu.CompilerParams(vmem_limit_bytes=60 * 1024 * 1024)


def forward_kernel(map_ref, obj_ref, kc_ref, ks_ref, out_ref):
    depth, rows, width = map_ref.shape
    half = width // 2
    band = kc_ref.shape[0] // depth
    maps = map_ref[...].astype(jnp.float32)
    obj = obj_ref[...].astype(jnp.float32)
    m_re, m_im = maps[..., :half], maps[..., half:]
    o_re, o_im = obj[..., :half], obj[..., half:]
    image = jnp.concatenate([m_re * o_re - m_im * o_im, m_re * o_im + m_im * o_re], axis=-1)
    pieces = []
    for h in range(rows // band):
        part = image[:, h * band : (h + 1) * band, :].reshape(depth * band, width)
        part = part.astype(jnp.bfloat16)
        direct = dot32(kc_ref[...], part)
        crossed = dot32(ks_ref[...], part)
        along_z = turn_add(direct, crossed, half).astype(jnp.bfloat16).astype(jnp.float32)
        pieces.append(along_z.reshape(depth, band, width))
    along_z = jnp.concatenate(pieces, axis=1).astype(jnp.bfloat16)
    out_ref[...] = along_z.reshape(out_ref.shape)


def line_kernel(in_ref, mask_ref, fx_ref, fxi_ref, wf_ref, wi_ref, out_ref):
    groups, rows, width = in_ref.shape
    half = width // 2
    lines = groups * rows
    volume = dot32(in_ref[...].reshape(lines, width), fx_ref[...]).astype(jnp.bfloat16)
    stacked = jnp.concatenate([volume[:, :half], volume[:, half:]], axis=0)
    spectrum = dot32(wf_ref[...], stacked).astype(jnp.bfloat16)
    flags = mask_ref[...]
    segments = flags.shape[1]
    segment = half // segments
    keep = jnp.concatenate(
        [jnp.broadcast_to(flags[:, s : s + 1], (lines, segment)) for s in range(segments)], axis=1
    )
    keep = jnp.concatenate([keep, keep], axis=0) > 0
    sampled = jnp.where(keep, spectrum, jnp.zeros_like(spectrum))
    back = dot32(wi_ref[...], sampled).astype(jnp.bfloat16)
    result = jnp.concatenate([back[:lines], back[lines:]], axis=1)
    result = dot32(result, fxi_ref[...]).astype(jnp.bfloat16)
    out_ref[...] = result.reshape(out_ref.shape)


def backward_kernel(first, last, in_ref, map_ref, kc_ref, ks_ref, *refs):
    depth, rows, width = map_ref.shape
    half = width // 2
    band = kc_ref.shape[0] // depth
    volume = in_ref[...].reshape(depth, rows, width).astype(jnp.float32)
    maps = map_ref[...].astype(jnp.float32)
    pieces = []
    for h in range(rows // band):
        part = volume[:, h * band : (h + 1) * band, :].reshape(depth * band, width)
        part = part.astype(jnp.bfloat16)
        direct = dot32(kc_ref[...], part)
        crossed = dot32(ks_ref[...], part)
        back_x = turn_add(direct, crossed, half).astype(jnp.bfloat16).astype(jnp.float32)
        coil = maps[:, h * band : (h + 1) * band, :].reshape(depth * band, width)
        m_re, m_im = coil[:, :half], coil[:, half:]
        b_re, b_im = back_x[:, :half], back_x[:, half:]
        piece = jnp.concatenate(
            [m_re * b_re + m_im * b_im, m_re * b_im - m_im * b_re], axis=1
        )
        pieces.append(piece.reshape(depth, band, width))
    product = jnp.concatenate(pieces, axis=1)
    refs = list(refs)
    acc_ref = None if first else refs.pop(0)
    out_ref = refs.pop(0)
    sum_ref = refs.pop(0) if last else out_ref
    step = pl.program_id(0)

    @pl.when(step == 0)
    def _():
        sum_ref[...] = product if first else acc_ref[...] + product

    @pl.when(step > 0)
    def _():
        sum_ref[...] += product

    if last:
        @pl.when(step == pl.num_programs(0) - 1)
        def _():
            out_ref[...] = sum_ref[...].astype(out_ref.dtype)


def on_device(object_image, coil_maps, sample_mask):
    width = object_image.shape[2]
    readout = width // 2
    slices, rows = object_image.shape[0], object_image.shape[1]
    coils = coil_maps.shape[0]
    pencils = lax.axis_size("pencil")
    depth = slices // pencils
    lines = rows * pencils
    position = lax.axis_index("pencil")

    cos_x, sin_x = complex_tables(readout)
    forward_x = readout_table(cos_x, sin_x)
    inverse_x = readout_table(cos_x, -sin_x)
    band = 8 if rows % 8 == 0 else rows
    kc_f, ks_f = slice_tables(slices, -1.0, band)
    kc_i, ks_i = slice_tables(slices, 1.0, band)
    cos_y, sin_y = complex_tables(lines)
    wf = block_table(cos_y, sin_y)
    wi = block_table(cos_y, -sin_y)
    mask = lax.dynamic_slice_in_dim(sample_mask, position * depth, depth, 0)

    tail = coils // 2
    sizes = [coils - tail, tail] if tail > 0 else [coils]
    const2 = lambda c: (0, 0)
    const3 = lambda c: (0, 0, 0)
    acc = None
    start = 0
    for per in sizes:
        map_spec = pl.BlockSpec((None, slices, rows, width), lambda c, s=start: (c + s, 0, 0, 0))
        split = pl.pallas_call(
            forward_kernel,
            grid=(per,),
            in_specs=[
                map_spec,
                pl.BlockSpec((slices, rows, width), const3),
                pl.BlockSpec((slices * band, slices * band), const2),
                pl.BlockSpec((slices * band, slices * band), const2),
            ],
            out_specs=pl.BlockSpec(
                (pencils, None, depth, rows, width), lambda c: (0, c, 0, 0, 0)
            ),
            out_shape=jax.ShapeDtypeStruct((pencils, per, depth, rows, width), jnp.bfloat16),
            compiler_params=PARAMS,
        )(coil_maps, object_image, kc_f, ks_f)
        gathered = lax.all_to_all(split, "pencil", 0, 0, tiled=True)
        lined = pl.pallas_call(
            line_kernel,
            grid=(per, depth),
            in_specs=[
                pl.BlockSpec((pencils, None, None, rows, width), lambda c, k: (0, c, k, 0, 0)),
                pl.BlockSpec((None, lines, sample_mask.shape[2]), lambda c, k: (k, 0, 0)),
                pl.BlockSpec((width, width), lambda c, k: (0, 0)),
                pl.BlockSpec((width, width), lambda c, k: (0, 0)),
                pl.BlockSpec((2 * lines, 2 * lines), lambda c, k: (0, 0)),
                pl.BlockSpec((2 * lines, 2 * lines), lambda c, k: (0, 0)),
            ],
            out_specs=pl.BlockSpec(
                (pencils, None, None, rows, width), lambda c, k: (0, c, k, 0, 0)
            ),
            out_shape=jax.ShapeDtypeStruct((pencils, per, depth, rows, width), jnp.bfloat16),
            compiler_params=PARAMS,
        )(gathered, mask, forward_x, inverse_x, wf, wi)
        returned = lax.all_to_all(lined, "pencil", 0, 0, tiled=True)
        first, last = start == 0, start + per == coils
        operands = [returned, coil_maps, kc_i, ks_i]
        in_specs = [
            pl.BlockSpec((pencils, None, depth, rows, width), lambda c: (0, c, 0, 0, 0)),
            map_spec,
            pl.BlockSpec((slices * band, slices * band), const2),
            pl.BlockSpec((slices * band, slices * band), const2),
        ]
        if not first:
            operands.append(acc)
            in_specs.append(pl.BlockSpec((slices, rows, width), const3))
        acc = pl.pallas_call(
            functools.partial(backward_kernel, first, last),
            grid=(per,),
            in_specs=in_specs,
            out_specs=pl.BlockSpec((slices, rows, width), const3),
            out_shape=jax.ShapeDtypeStruct(
                (slices, rows, width), jnp.bfloat16 if last else jnp.float32
            ),
            scratch_shapes=[pltpu.VMEM((slices, rows, width), jnp.float32)] if last else [],
            compiler_params=pltpu.CompilerParams(
                vmem_limit_bytes=60 * 1024 * 1024, dimension_semantics=("arbitrary",)
            ),
        )(*operands)
        start += per
    groups = lax.axis_size("coil")
    parts = acc.reshape(groups, slices // groups, rows, width)
    parts = lax.all_to_all(parts, "coil", 0, 0, tiled=True)
    return jnp.sum(parts.astype(jnp.float32), axis=0)


def solution(mesh):
    placed = (P(None, "pencil", None), P("coil", None, "pencil", None), P())
    return jax.shard_map(
        on_device, mesh=mesh, in_specs=placed, out_specs=P("coil", "pencil", None), check_vma=False
    )
```

```python
import functools
import math

import jax
import ml_dtypes
import numpy as np
import jax.numpy as jnp
from jax import lax
from jax.experimental import pallas as pl
from jax.experimental.pallas import tpu as pltpu
from jax.sharding import PartitionSpec as P


def dft_tables(length, direction):
    indices = np.arange(length, dtype=np.int32)
    phases = indices[:, None] * indices[None, :] % length
    angles = phases.astype(np.float32) * np.float32(2.0 * math.pi / length)
    factor = np.float32(1.0 / math.sqrt(length))
    cosine = (np.cos(angles) * factor).astype(ml_dtypes.bfloat16)
    sine_part = (np.float32(direction) * np.sin(angles) * factor).astype(ml_dtypes.bfloat16)
    return (cosine, sine_part)


def complex_tables(length):
    cosine, sine_part = dft_tables(length, -1.0)
    return lax.optimization_barrier((jnp.asarray(cosine), jnp.asarray(sine_part)))


def readout_table(cosine, sine_part):
    upper = jnp.concatenate([cosine, sine_part], axis=1)
    lower = jnp.concatenate([-sine_part, cosine], axis=1)
    return jnp.concatenate([upper, lower], axis=0)


def block_table(cosine, sine_part):
    upper = jnp.concatenate([cosine, -sine_part], axis=1)
    lower = jnp.concatenate([sine_part, cosine], axis=1)
    return jnp.concatenate([upper, lower], axis=0)


def slice_tables(length, direction, rows):
    cosine, sine_part = dft_tables(length, direction)
    eye = np.eye(rows, dtype=np.float32)
    kron = lambda t: jnp.asarray(np.kron(t.astype(np.float32), eye).astype(ml_dtypes.bfloat16))
    return kron(cosine), kron(sine_part)


def turn_add(direct, crossed, half):
    return jnp.concatenate(
        [direct[:, :half] - crossed[:, half:], direct[:, half:] + crossed[:, :half]], axis=1
    )


def dot32(a, b):
    return jnp.dot(a, b, preferred_element_type=jnp.float32)


PARAMS = pltpu.CompilerParams(vmem_limit_bytes=60 * 1024 * 1024)


def forward_kernel(map_ref, obj_ref, kc_ref, ks_ref, out_ref):
    depth, rows, width = map_ref.shape
    half = width // 2
    band = kc_ref.shape[0] // depth
    maps = map_ref[...].astype(jnp.float32)
    obj = obj_ref[...].astype(jnp.float32)
    m_re, m_im = maps[..., :half], maps[..., half:]
    o_re, o_im = obj[..., :half], obj[..., half:]
    image = jnp.concatenate([m_re * o_re - m_im * o_im, m_re * o_im + m_im * o_re], axis=-1)
    pieces = []
    for h in range(rows // band):
        part = image[:, h * band : (h + 1) * band, :].reshape(depth * band, width)
        part = part.astype(jnp.bfloat16)
        direct = dot32(kc_ref[...], part)
        crossed = dot32(ks_ref[...], part)
        along_z = turn_add(direct, crossed, half).astype(jnp.bfloat16).astype(jnp.float32)
        pieces.append(along_z.reshape(depth, band, width))
    along_z = jnp.concatenate(pieces, axis=1).astype(jnp.bfloat16)
    out_ref[...] = along_z.reshape(out_ref.shape)


def line_kernel(in_ref, mask_ref, fx_ref, fxi_ref, wf_ref, wi_ref, out_ref):
    groups, rows, width = in_ref.shape
    half = width // 2
    lines = groups * rows
    volume = dot32(in_ref[...].reshape(lines, width), fx_ref[...]).astype(jnp.bfloat16)
    stacked = jnp.concatenate([volume[:, :half], volume[:, half:]], axis=0)
    spectrum = dot32(wf_ref[...], stacked).astype(jnp.bfloat16)
    flags = mask_ref[...]
    segments = flags.shape[1]
    segment = half // segments
    keep = jnp.concatenate(
        [jnp.broadcast_to(flags[:, s : s + 1], (lines, segment)) for s in range(segments)], axis=1
    )
    keep = jnp.concatenate([keep, keep], axis=0) > 0
    sampled = jnp.where(keep, spectrum, jnp.zeros_like(spectrum))
    back = dot32(wi_ref[...], sampled).astype(jnp.bfloat16)
    result = jnp.concatenate([back[:lines], back[lines:]], axis=1)
    result = dot32(result, fxi_ref[...]).astype(jnp.bfloat16)
    out_ref[...] = result.reshape(out_ref.shape)


def backward_kernel(first, last, in_ref, map_ref, kc_ref, ks_ref, *refs):
    depth, rows, width = map_ref.shape
    half = width // 2
    band = kc_ref.shape[0] // depth
    volume = in_ref[...].reshape(depth, rows, width).astype(jnp.float32)
    maps = map_ref[...].astype(jnp.float32)
    pieces = []
    for h in range(rows // band):
        part = volume[:, h * band : (h + 1) * band, :].reshape(depth * band, width)
        part = part.astype(jnp.bfloat16)
        direct = dot32(kc_ref[...], part)
        crossed = dot32(ks_ref[...], part)
        back_x = turn_add(direct, crossed, half).astype(jnp.bfloat16).astype(jnp.float32)
        coil = maps[:, h * band : (h + 1) * band, :].reshape(depth * band, width)
        m_re, m_im = coil[:, :half], coil[:, half:]
        b_re, b_im = back_x[:, :half], back_x[:, half:]
        piece = jnp.concatenate(
            [m_re * b_re + m_im * b_im, m_re * b_im - m_im * b_re], axis=1
        )
        pieces.append(piece.reshape(depth, band, width))
    product = jnp.concatenate(pieces, axis=1)
    refs = list(refs)
    acc_ref = None if first else refs.pop(0)
    out_ref = refs.pop(0)
    sum_ref = refs.pop(0) if last else out_ref
    step = pl.program_id(0)

    @pl.when(step == 0)
    def _():
        sum_ref[...] = product if first else acc_ref[...] + product

    @pl.when(step > 0)
    def _():
        sum_ref[...] += product

    if last:
        @pl.when(step == pl.num_programs(0) - 1)
        def _():
            out_ref[...] = sum_ref[...].astype(out_ref.dtype)


def on_device(object_image, coil_maps, sample_mask):
    width = object_image.shape[2]
    readout = width // 2
    slices, rows = object_image.shape[0], object_image.shape[1]
    coils = coil_maps.shape[0]
    pencils = lax.axis_size("pencil")
    depth = slices // pencils
    lines = rows * pencils
    position = lax.axis_index("pencil")

    band = 8 if rows % 8 == 0 else rows
    kc_f, ks_f = slice_tables(slices, -1.0, band)
    kc_i, ks_i = slice_tables(slices, 1.0, band)
    mask = lax.dynamic_slice_in_dim(sample_mask, position * depth, depth, 0)

    tail = coils // 4
    sizes = [coils - tail, tail] if tail > 0 else [coils]
    const2 = lambda c: (0, 0)
    const3 = lambda c: (0, 0, 0)
    splits = []
    start = 0
    for per in sizes:
        map_spec = pl.BlockSpec((None, slices, rows, width), lambda c, s=start: (c + s, 0, 0, 0))
        splits.append(pl.pallas_call(
            forward_kernel,
            grid=(per,),
            in_specs=[
                map_spec,
                pl.BlockSpec((slices, rows, width), const3),
                pl.BlockSpec((slices * band, slices * band), const2),
                pl.BlockSpec((slices * band, slices * band), const2),
            ],
            out_specs=pl.BlockSpec(
                (pencils, None, depth, rows, width), lambda c: (0, c, 0, 0, 0)
            ),
            out_shape=jax.ShapeDtypeStruct((pencils, per, depth, rows, width), jnp.bfloat16),
            compiler_params=PARAMS,
        )(coil_maps, object_image, kc_f, ks_f))
        start += per

    cos_x, sin_x = complex_tables(readout)
    cos_y, sin_y = complex_tables(lines)
    forward_x = readout_table(cos_x, sin_x)
    inverse_x = readout_table(cos_x, -sin_x)
    wf = block_table(cos_y, sin_y)
    wi = block_table(cos_y, -sin_y)
    forward_x, inverse_x, wf, wi, splits[-1] = lax.optimization_barrier(
        (forward_x, inverse_x, wf, wi, splits[-1])
    )
    volumes = [lax.all_to_all(split, "pencil", 0, 0, tiled=True) for split in splits]

    acc = None
    start = 0
    for per, gathered in zip(sizes, volumes):
        map_spec = pl.BlockSpec((None, slices, rows, width), lambda c, s=start: (c + s, 0, 0, 0))
        lined = pl.pallas_call(
            line_kernel,
            grid=(per, depth),
            in_specs=[
                pl.BlockSpec((pencils, None, None, rows, width), lambda c, k: (0, c, k, 0, 0)),
                pl.BlockSpec((None, lines, sample_mask.shape[2]), lambda c, k: (k, 0, 0)),
                pl.BlockSpec((width, width), lambda c, k: (0, 0)),
                pl.BlockSpec((width, width), lambda c, k: (0, 0)),
                pl.BlockSpec((2 * lines, 2 * lines), lambda c, k: (0, 0)),
                pl.BlockSpec((2 * lines, 2 * lines), lambda c, k: (0, 0)),
            ],
            out_specs=pl.BlockSpec(
                (pencils, None, None, rows, width), lambda c, k: (0, c, k, 0, 0)
            ),
            out_shape=jax.ShapeDtypeStruct((pencils, per, depth, rows, width), jnp.bfloat16),
            compiler_params=PARAMS,
        )(gathered, mask, forward_x, inverse_x, wf, wi)
        returned = lax.all_to_all(lined, "pencil", 0, 0, tiled=True)
        first, last = start == 0, start + per == coils
        operands = [returned, coil_maps, kc_i, ks_i]
        in_specs = [
            pl.BlockSpec((pencils, None, depth, rows, width), lambda c: (0, c, 0, 0, 0)),
            map_spec,
            pl.BlockSpec((slices * band, slices * band), const2),
            pl.BlockSpec((slices * band, slices * band), const2),
        ]
        if not first:
            operands.append(acc)
            in_specs.append(pl.BlockSpec((slices, rows, width), const3))
        acc = pl.pallas_call(
            functools.partial(backward_kernel, first, last),
            grid=(per,),
            in_specs=in_specs,
            out_specs=pl.BlockSpec((slices, rows, width), const3),
            out_shape=jax.ShapeDtypeStruct(
                (slices, rows, width), jnp.bfloat16 if last else jnp.float32
            ),
            scratch_shapes=[pltpu.VMEM((slices, rows, width), jnp.float32)] if last else [],
            compiler_params=pltpu.CompilerParams(
                vmem_limit_bytes=60 * 1024 * 1024, dimension_semantics=("arbitrary",)
            ),
        )(*operands)
        start += per
    groups = lax.axis_size("coil")
    parts = acc.reshape(groups, slices // groups, rows, width)
    parts = lax.all_to_all(parts, "coil", 0, 0, tiled=True)
    return jnp.sum(parts.astype(jnp.float32), axis=0)


def solution(mesh):
    placed = (P(None, "pencil", None), P("coil", None, "pencil", None), P())
    return jax.shard_map(
        on_device, mesh=mesh, in_specs=placed, out_specs=P("coil", "pencil", None), check_vma=False
    )
```

```python
import functools
import math

import jax
import ml_dtypes
import numpy as np
import jax.numpy as jnp
from jax import lax
from jax.experimental import pallas as pl
from jax.experimental.pallas import tpu as pltpu
from jax.sharding import PartitionSpec as P


def dft_tables(length, direction):
    indices = np.arange(length, dtype=np.int32)
    phases = indices[:, None] * indices[None, :] % length
    angles = phases.astype(np.float32) * np.float32(2.0 * math.pi / length)
    factor = np.float32(1.0 / math.sqrt(length))
    cosine = (np.cos(angles) * factor).astype(ml_dtypes.bfloat16)
    sine_part = (np.float32(direction) * np.sin(angles) * factor).astype(ml_dtypes.bfloat16)
    return (cosine, sine_part)


def complex_tables(length):
    cosine, sine_part = dft_tables(length, -1.0)
    return lax.optimization_barrier((jnp.asarray(cosine), jnp.asarray(sine_part)))


def readout_table(cosine, sine_part):
    upper = jnp.concatenate([cosine, sine_part], axis=1)
    lower = jnp.concatenate([-sine_part, cosine], axis=1)
    return jnp.concatenate([upper, lower], axis=0)


def block_table(cosine, sine_part):
    upper = jnp.concatenate([cosine, -sine_part], axis=1)
    lower = jnp.concatenate([sine_part, cosine], axis=1)
    return jnp.concatenate([upper, lower], axis=0)


def slice_tables(length, direction, rows):
    cosine, sine_part = dft_tables(length, direction)
    eye = np.eye(rows, dtype=np.float32)
    kron = lambda t: jnp.asarray(np.kron(t.astype(np.float32), eye).astype(ml_dtypes.bfloat16))
    return kron(cosine), kron(sine_part)


def turn_add(direct, crossed, half):
    return jnp.concatenate(
        [direct[:, :half] - crossed[:, half:], direct[:, half:] + crossed[:, :half]], axis=1
    )


def dot32(a, b):
    return jnp.dot(a, b, preferred_element_type=jnp.float32)


PARAMS = pltpu.CompilerParams(vmem_limit_bytes=60 * 1024 * 1024)


def forward_kernel(map_ref, obj_ref, kc_ref, ks_ref, out_ref):
    depth, rows, width = map_ref.shape
    half = width // 2
    band = kc_ref.shape[0] // depth
    maps = map_ref[...].astype(jnp.float32)
    obj = obj_ref[...].astype(jnp.float32)
    m_re, m_im = maps[..., :half], maps[..., half:]
    o_re, o_im = obj[..., :half], obj[..., half:]
    image = jnp.concatenate([m_re * o_re - m_im * o_im, m_re * o_im + m_im * o_re], axis=-1)
    for h in range(rows // band):
        part = image[:, h * band : (h + 1) * band, :].reshape(depth * band, width)
        part = part.astype(jnp.bfloat16)
        direct = dot32(kc_ref[...], part)
        crossed = dot32(ks_ref[...], part)
        along_z = turn_add(direct, crossed, half).astype(jnp.bfloat16)
        out_ref[:, :, h * band : (h + 1) * band, :] = along_z.reshape(
            out_ref.shape[:2] + (band, width)
        )


def line_kernel(in_ref, mask_ref, fx_ref, fxi_ref, wf_ref, wi_ref, out_ref):
    groups, rows, width = in_ref.shape
    half = width // 2
    lines = groups * rows
    volume = dot32(in_ref[...].reshape(lines, width), fx_ref[...]).astype(jnp.bfloat16)
    stacked = jnp.concatenate([volume[:, :half], volume[:, half:]], axis=0)
    spectrum = dot32(wf_ref[...], stacked).astype(jnp.bfloat16)
    flags = mask_ref[...]
    segments = flags.shape[1]
    segment = half // segments
    keep = jnp.concatenate(
        [jnp.broadcast_to(flags[:, s : s + 1], (lines, segment)) for s in range(segments)], axis=1
    )
    keep = jnp.concatenate([keep, keep], axis=0) > 0
    sampled = jnp.where(keep, spectrum, jnp.zeros_like(spectrum))
    back = dot32(wi_ref[...], sampled).astype(jnp.bfloat16)
    result = jnp.concatenate([back[:lines], back[lines:]], axis=1)
    result = dot32(result, fxi_ref[...]).astype(jnp.bfloat16)
    out_ref[...] = result.reshape(out_ref.shape)


def backward_kernel(first, last, in_ref, map_ref, kc_ref, ks_ref, *refs):
    depth, rows, width = map_ref.shape
    half = width // 2
    band = kc_ref.shape[0] // depth
    maps = map_ref[...].astype(jnp.float32)
    pieces = []
    for h in range(rows // band):
        part = in_ref[:, :, h * band : (h + 1) * band, :].reshape(depth * band, width)
        direct = dot32(kc_ref[...], part)
        crossed = dot32(ks_ref[...], part)
        back_x = turn_add(direct, crossed, half).astype(jnp.bfloat16).astype(jnp.float32)
        coil = maps[:, h * band : (h + 1) * band, :].reshape(depth * band, width)
        m_re, m_im = coil[:, :half], coil[:, half:]
        b_re, b_im = back_x[:, :half], back_x[:, half:]
        piece = jnp.concatenate(
            [m_re * b_re + m_im * b_im, m_re * b_im - m_im * b_re], axis=1
        )
        pieces.append(piece.reshape(depth, band, width))
    product = jnp.concatenate(pieces, axis=1)
    refs = list(refs)
    acc_ref = None if first else refs.pop(0)
    out_ref = refs.pop(0)
    sum_ref = refs.pop(0) if last else out_ref
    step = pl.program_id(0)

    @pl.when(step == 0)
    def _():
        sum_ref[...] = product if first else acc_ref[...] + product

    @pl.when(step > 0)
    def _():
        sum_ref[...] += product

    if last:
        @pl.when(step == pl.num_programs(0) - 1)
        def _():
            out_ref[...] = sum_ref[...].astype(out_ref.dtype)


def on_device(object_image, coil_maps, sample_mask):
    width = object_image.shape[2]
    readout = width // 2
    slices, rows = object_image.shape[0], object_image.shape[1]
    coils = coil_maps.shape[0]
    pencils = lax.axis_size("pencil")
    depth = slices // pencils
    lines = rows * pencils
    position = lax.axis_index("pencil")

    cos_x, sin_x = complex_tables(readout)
    forward_x = readout_table(cos_x, sin_x)
    inverse_x = readout_table(cos_x, -sin_x)
    band = 8 if rows % 8 == 0 else rows
    kc_f, ks_f = slice_tables(slices, -1.0, band)
    kc_i, ks_i = slice_tables(slices, 1.0, band)
    cos_y, sin_y = complex_tables(lines)
    wf = block_table(cos_y, sin_y)
    wi = block_table(cos_y, -sin_y)
    mask = lax.dynamic_slice_in_dim(sample_mask, position * depth, depth, 0)

    tail = coils // 2
    sizes = [coils - tail, tail] if tail > 0 else [coils]
    const2 = lambda c: (0, 0)
    const3 = lambda c: (0, 0, 0)
    acc = None
    start = 0
    for per in sizes:
        map_spec = pl.BlockSpec((None, slices, rows, width), lambda c, s=start: (c + s, 0, 0, 0))
        split = pl.pallas_call(
            forward_kernel,
            grid=(per,),
            in_specs=[
                map_spec,
                pl.BlockSpec((slices, rows, width), const3),
                pl.BlockSpec((slices * band, slices * band), const2),
                pl.BlockSpec((slices * band, slices * band), const2),
            ],
            out_specs=pl.BlockSpec(
                (pencils, None, depth, rows, width), lambda c: (0, c, 0, 0, 0)
            ),
            out_shape=jax.ShapeDtypeStruct((pencils, per, depth, rows, width), jnp.bfloat16),
            compiler_params=PARAMS,
        )(coil_maps, object_image, kc_f, ks_f)
        gathered = lax.all_to_all(split, "pencil", 0, 0, tiled=True)
        lined = pl.pallas_call(
            line_kernel,
            grid=(per, depth),
            in_specs=[
                pl.BlockSpec((pencils, None, None, rows, width), lambda c, k: (0, c, k, 0, 0)),
                pl.BlockSpec((None, lines, sample_mask.shape[2]), lambda c, k: (k, 0, 0)),
                pl.BlockSpec((width, width), lambda c, k: (0, 0)),
                pl.BlockSpec((width, width), lambda c, k: (0, 0)),
                pl.BlockSpec((2 * lines, 2 * lines), lambda c, k: (0, 0)),
                pl.BlockSpec((2 * lines, 2 * lines), lambda c, k: (0, 0)),
            ],
            out_specs=pl.BlockSpec(
                (pencils, None, None, rows, width), lambda c, k: (0, c, k, 0, 0)
            ),
            out_shape=jax.ShapeDtypeStruct((pencils, per, depth, rows, width), jnp.bfloat16),
            compiler_params=PARAMS,
        )(gathered, mask, forward_x, inverse_x, wf, wi)
        returned = lax.all_to_all(lined, "pencil", 0, 0, tiled=True)
        first, last = start == 0, start + per == coils
        operands = [returned, coil_maps, kc_i, ks_i]
        in_specs = [
            pl.BlockSpec((pencils, None, depth, rows, width), lambda c: (0, c, 0, 0, 0)),
            map_spec,
            pl.BlockSpec((slices * band, slices * band), const2),
            pl.BlockSpec((slices * band, slices * band), const2),
        ]
        if not first:
            operands.append(acc)
            in_specs.append(pl.BlockSpec((slices, rows, width), const3))
        acc = pl.pallas_call(
            functools.partial(backward_kernel, first, last),
            grid=(per,),
            in_specs=in_specs,
            out_specs=pl.BlockSpec((slices, rows, width), const3),
            out_shape=jax.ShapeDtypeStruct(
                (slices, rows, width), jnp.bfloat16 if last else jnp.float32
            ),
            scratch_shapes=[pltpu.VMEM((slices, rows, width), jnp.float32)] if last else [],
            compiler_params=pltpu.CompilerParams(
                vmem_limit_bytes=60 * 1024 * 1024, dimension_semantics=("arbitrary",)
            ),
        )(*operands)
        start += per
    groups = lax.axis_size("coil")
    parts = acc.reshape(groups, slices // groups, rows, width)
    parts = lax.all_to_all(parts, "coil", 0, 0, tiled=True)
    return jnp.sum(parts.astype(jnp.float32), axis=0)


def solution(mesh):
    placed = (P(None, "pencil", None), P("coil", None, "pencil", None), P())
    return jax.shard_map(
        on_device, mesh=mesh, in_specs=placed, out_specs=P("coil", "pencil", None), check_vma=False
    )
```

```python
import functools
import math

import jax
import ml_dtypes
import numpy as np
import jax.numpy as jnp
from jax import lax
from jax.experimental import pallas as pl
from jax.experimental.pallas import tpu as pltpu
from jax.sharding import PartitionSpec as P


def dft_tables(length, direction):
    indices = np.arange(length, dtype=np.int32)
    phases = indices[:, None] * indices[None, :] % length
    angles = phases.astype(np.float32) * np.float32(2.0 * math.pi / length)
    factor = np.float32(1.0 / math.sqrt(length))
    cosine = (np.cos(angles) * factor).astype(ml_dtypes.bfloat16)
    sine_part = (np.float32(direction) * np.sin(angles) * factor).astype(ml_dtypes.bfloat16)
    return (cosine, sine_part)


def complex_tables(length):
    cosine, sine_part = dft_tables(length, -1.0)
    return lax.optimization_barrier((jnp.asarray(cosine), jnp.asarray(sine_part)))


def readout_table(cosine, sine_part):
    upper = jnp.concatenate([cosine, sine_part], axis=1)
    lower = jnp.concatenate([-sine_part, cosine], axis=1)
    return jnp.concatenate([upper, lower], axis=0)


def block_table(cosine, sine_part):
    upper = jnp.concatenate([cosine, -sine_part], axis=1)
    lower = jnp.concatenate([sine_part, cosine], axis=1)
    return jnp.concatenate([upper, lower], axis=0)


def slice_tables(length, direction, rows):
    cosine, sine_part = dft_tables(length, direction)
    eye = np.eye(rows, dtype=np.float32)
    kron = lambda t: jnp.asarray(np.kron(t.astype(np.float32), eye).astype(ml_dtypes.bfloat16))
    return kron(cosine), kron(sine_part)


def turn_add(direct, crossed, half):
    return jnp.concatenate(
        [direct[:, :half] - crossed[:, half:], direct[:, half:] + crossed[:, :half]], axis=1
    )


def dot32(a, b):
    return jnp.dot(a, b, preferred_element_type=jnp.float32)


PARAMS = pltpu.CompilerParams(vmem_limit_bytes=60 * 1024 * 1024)


def forward_kernel(map_ref, obj_ref, k_ref, out_ref):
    depth, rows, width = map_ref.shape
    half = width // 2
    band = k_ref.shape[1] // depth
    lines = depth * band
    maps = map_ref[...].astype(jnp.float32)
    obj = obj_ref[...].astype(jnp.float32)
    m_re, m_im = maps[..., :half], maps[..., half:]
    o_re, o_im = obj[..., :half], obj[..., half:]
    image = jnp.concatenate([m_re * o_re - m_im * o_im, m_re * o_im + m_im * o_re], axis=-1)
    for h in range(rows // band):
        part = image[:, h * band : (h + 1) * band, :].reshape(depth * band, width)
        part = part.astype(jnp.bfloat16)
        both = dot32(k_ref[...], part)
        direct, crossed = both[:lines], both[lines:]
        along_z = turn_add(direct, crossed, half).astype(jnp.bfloat16)
        out_ref[:, :, h * band : (h + 1) * band, :] = along_z.reshape(
            out_ref.shape[:2] + (band, width)
        )


def line_kernel(in_ref, mask_ref, fx_ref, fxi_ref, wf_ref, wi_ref, out_ref):
    groups, rows, width = in_ref.shape
    half = width // 2
    lines = groups * rows
    volume = dot32(in_ref[...].reshape(lines, width), fx_ref[...]).astype(jnp.bfloat16)
    stacked = jnp.concatenate([volume[:, :half], volume[:, half:]], axis=0)
    spectrum = dot32(wf_ref[...], stacked).astype(jnp.bfloat16)
    flags = mask_ref[...]
    segments = flags.shape[1]
    segment = half // segments
    keep = jnp.concatenate(
        [jnp.broadcast_to(flags[:, s : s + 1], (lines, segment)) for s in range(segments)], axis=1
    )
    keep = jnp.concatenate([keep, keep], axis=0) > 0
    sampled = jnp.where(keep, spectrum, jnp.zeros_like(spectrum))
    back = dot32(wi_ref[...], sampled).astype(jnp.bfloat16)
    result = jnp.concatenate([back[:lines], back[lines:]], axis=1)
    result = dot32(result, fxi_ref[...]).astype(jnp.bfloat16)
    out_ref[...] = result.reshape(out_ref.shape)


def backward_kernel(first, last, in_ref, map_ref, k_ref, *refs):
    depth, rows, width = map_ref.shape
    half = width // 2
    band = k_ref.shape[1] // depth
    lines = depth * band
    maps = map_ref[...].astype(jnp.float32)
    pieces = []
    for h in range(rows // band):
        part = in_ref[:, :, h * band : (h + 1) * band, :].reshape(depth * band, width)
        both = dot32(k_ref[...], part)
        direct, crossed = both[:lines], both[lines:]
        back_x = turn_add(direct, crossed, half).astype(jnp.bfloat16).astype(jnp.float32)
        coil = maps[:, h * band : (h + 1) * band, :].reshape(depth * band, width)
        m_re, m_im = coil[:, :half], coil[:, half:]
        b_re, b_im = back_x[:, :half], back_x[:, half:]
        piece = jnp.concatenate(
            [m_re * b_re + m_im * b_im, m_re * b_im - m_im * b_re], axis=1
        )
        pieces.append(piece.reshape(depth, band, width))
    product = jnp.concatenate(pieces, axis=1)
    refs = list(refs)
    acc_ref = None if first else refs.pop(0)
    out_ref = refs.pop(0)
    sum_ref = refs.pop(0) if last else out_ref
    step = pl.program_id(0)

    @pl.when(step == 0)
    def _():
        sum_ref[...] = product if first else acc_ref[...] + product

    @pl.when(step > 0)
    def _():
        sum_ref[...] += product

    if last:
        @pl.when(step == pl.num_programs(0) - 1)
        def _():
            out_ref[...] = sum_ref[...].astype(out_ref.dtype)


def on_device(object_image, coil_maps, sample_mask):
    width = object_image.shape[2]
    readout = width // 2
    slices, rows = object_image.shape[0], object_image.shape[1]
    coils = coil_maps.shape[0]
    pencils = lax.axis_size("pencil")
    depth = slices // pencils
    lines = rows * pencils
    position = lax.axis_index("pencil")

    cos_x, sin_x = complex_tables(readout)
    forward_x = readout_table(cos_x, sin_x)
    inverse_x = readout_table(cos_x, -sin_x)
    band = 8 if rows % 8 == 0 else rows
    k_f = jnp.concatenate(slice_tables(slices, -1.0, band), axis=0)
    k_i = jnp.concatenate(slice_tables(slices, 1.0, band), axis=0)
    cos_y, sin_y = complex_tables(lines)
    wf = block_table(cos_y, sin_y)
    wi = block_table(cos_y, -sin_y)
    mask = lax.dynamic_slice_in_dim(sample_mask, position * depth, depth, 0)

    tail = coils // 2
    sizes = [coils - tail, tail] if tail > 0 else [coils]
    const2 = lambda c: (0, 0)
    const3 = lambda c: (0, 0, 0)
    acc = None
    start = 0
    for per in sizes:
        map_spec = pl.BlockSpec((None, slices, rows, width), lambda c, s=start: (c + s, 0, 0, 0))
        split = pl.pallas_call(
            forward_kernel,
            grid=(per,),
            in_specs=[
                map_spec,
                pl.BlockSpec((slices, rows, width), const3),
                pl.BlockSpec((2 * slices * band, slices * band), const2),
            ],
            out_specs=pl.BlockSpec(
                (pencils, None, depth, rows, width), lambda c: (0, c, 0, 0, 0)
            ),
            out_shape=jax.ShapeDtypeStruct((pencils, per, depth, rows, width), jnp.bfloat16),
            compiler_params=PARAMS,
        )(coil_maps, object_image, k_f)
        gathered = lax.all_to_all(split, "pencil", 0, 0, tiled=True)
        lined = pl.pallas_call(
            line_kernel,
            grid=(per, depth),
            in_specs=[
                pl.BlockSpec((pencils, None, None, rows, width), lambda c, k: (0, c, k, 0, 0)),
                pl.BlockSpec((None, lines, sample_mask.shape[2]), lambda c, k: (k, 0, 0)),
                pl.BlockSpec((width, width), lambda c, k: (0, 0)),
                pl.BlockSpec((width, width), lambda c, k: (0, 0)),
                pl.BlockSpec((2 * lines, 2 * lines), lambda c, k: (0, 0)),
                pl.BlockSpec((2 * lines, 2 * lines), lambda c, k: (0, 0)),
            ],
            out_specs=pl.BlockSpec(
                (pencils, None, None, rows, width), lambda c, k: (0, c, k, 0, 0)
            ),
            out_shape=jax.ShapeDtypeStruct((pencils, per, depth, rows, width), jnp.bfloat16),
            compiler_params=PARAMS,
        )(gathered, mask, forward_x, inverse_x, wf, wi)
        returned = lax.all_to_all(lined, "pencil", 0, 0, tiled=True)
        first, last = start == 0, start + per == coils
        operands = [returned, coil_maps, k_i]
        in_specs = [
            pl.BlockSpec((pencils, None, depth, rows, width), lambda c: (0, c, 0, 0, 0)),
            map_spec,
            pl.BlockSpec((2 * slices * band, slices * band), const2),
        ]
        if not first:
            operands.append(acc)
            in_specs.append(pl.BlockSpec((slices, rows, width), const3))
        acc = pl.pallas_call(
            functools.partial(backward_kernel, first, last),
            grid=(per,),
            in_specs=in_specs,
            out_specs=pl.BlockSpec((slices, rows, width), const3),
            out_shape=jax.ShapeDtypeStruct(
                (slices, rows, width), jnp.bfloat16 if last else jnp.float32
            ),
            scratch_shapes=[pltpu.VMEM((slices, rows, width), jnp.float32)] if last else [],
            compiler_params=pltpu.CompilerParams(
                vmem_limit_bytes=60 * 1024 * 1024, dimension_semantics=("arbitrary",)
            ),
        )(*operands)
        start += per
    groups = lax.axis_size("coil")
    parts = acc.reshape(groups, slices // groups, rows, width)
    parts = lax.all_to_all(parts, "coil", 0, 0, tiled=True)
    return jnp.sum(parts.astype(jnp.float32), axis=0)


def solution(mesh):
    placed = (P(None, "pencil", None), P("coil", None, "pencil", None), P())
    return jax.shard_map(
        on_device, mesh=mesh, in_specs=placed, out_specs=P("coil", "pencil", None), check_vma=False
    )
```
